512 devices in a mesh: dp: 2 (over core), section: 8 (over z), mem: 32 (over y, x).
Axes of the slice: x: 4, y: 8, z: 8, core: 2. Of those that a mesh axis runs over, the one named last changes fastest.
Arguments:
- qkv_rows: bfloat16 [8, 64, 128, 3072], P('section', ('dp', 'mem')), may hold values from -5 to 5
- grad_output: bfloat16 [8, 64, 128, 2048], P('section', ('dp', 'mem')), may hold values from -12 to 12
- memory_rows: bfloat16 [8, 256, 64, 1024], P('section', 'mem'), may hold values from -5 to 5
- shard_fill: int32 [8, 32], P('section', 'mem'), may hold values from 257 to 512, as said below
- block_ids: int32 [8, 64, 2, 8], P('section', ('dp', 'mem')), may hold values from 0 to 255, as said below
Outputs:
- upstream: bfloat16 [8, 64, 128, 3072], P('section', ('dp', 'mem'))
- memory_grad: bfloat16 [8, 256, 64, 1024], P('section', 'mem')
The draws below stay inside these ranges and needn't reach their ends.
Inputs may be any that keep to these rules, and one draw needn't show every extreme that they name: `shard_fill`: memory tokens at or beyond a shard's fill are empty. In every section one shard is full and one holds 257 tokens. `block_ids`: each query block names 8 blocks of different shards; all query blocks of one sequence together name at most one distinct block of any one shard; every named block holds a live token.
All inputs are finite; a program needn't handle non-finite values.
Results may differ from the reference program's by a relative error of at most 0.011.
Values may be sent and summed in bfloat16 or wider, within the bound.
No kernel may reach another device: no remote copies, remote signals or barrier semaphores. Data moves between devices by JAX's collectives and lax.ppermute only.
A program may use at most 128 MiB of HBM per device.

```python
import math
import jax
import jax.numpy as jnp
from jax import lax

H = 16
KEY_VALUE_HEADS = 4
DH = 128
BLK = 64
SEGMENT_TOKENS = 128
MB_DEV = 8
SECTION_COUNT = 8
SHARDS = 32
SEQUENCE_COUNT = 64
QB = 2
TOPK = 8
MEMBLOCKS = 256


def fill_table(key):
    key_short, key_order = jax.random.split(jax.random.fold_in(key, 11))
    half_len = MB_DEV * BLK // 2
    shortage = jax.random.randint(key_short, (SECTION_COUNT, SHARDS), 0, half_len)
    order = jax.vmap(lambda subkey: jax.random.permutation(subkey, SHARDS))(jax.random.split(key_order, SECTION_COUNT))
    shortage = jnp.where(order == 0, 0, shortage)
    shortage = jnp.where(order == 1, half_len - 1, shortage)
    return (MB_DEV * BLK - shortage).astype(jnp.int32)


def draw_shard_fill(key, part):
    return fill_table(key)


def draw_block_ids(key, part):
    fill_now = fill_table(key)
    live_blocks = (fill_now + BLK - 1) // BLK
    key_hot, key_coin, random_key_select, key_perm = jax.random.split(jax.random.fold_in(key, 23), 4)
    hot_block = jax.random.randint(key_hot, (SECTION_COUNT, SHARDS), 0, 1 << 20) % live_blocks
    coin_flip = jax.random.randint(key_coin, (SECTION_COUNT, SEQUENCE_COUNT, SHARDS), 0, 2)
    spread = jax.random.randint(random_key_select, (SECTION_COUNT, SEQUENCE_COUNT, SHARDS), 0, 1 << 20) % live_blocks[:, None, :]
    chosen = jnp.where(coin_flip == 1, hot_block[:, None, :], spread)
    perm_keys = jax.random.split(key_perm, SECTION_COUNT * SEQUENCE_COUNT * QB)
    owners = jax.vmap(lambda subkey: jax.random.permutation(subkey, SHARDS)[:TOPK])(perm_keys)
    owners = owners.reshape(SECTION_COUNT, SEQUENCE_COUNT, QB, TOPK)
    spread_full = jnp.broadcast_to(chosen[:, :, None, :], (SECTION_COUNT, SEQUENCE_COUNT, QB, SHARDS))
    local_pick = jnp.take_along_axis(spread_full, owners, axis=3)
    return (owners * MB_DEV + local_pick).astype(jnp.int32)


def draw_qkv_rows(key, part):
    random_key_root, random_key_queryscale = jax.random.split(jax.random.fold_in(key, 5), 2)
    shape = (SECTION_COUNT, SEQUENCE_COUNT, SEGMENT_TOKENS, H + 2 * KEY_VALUE_HEADS, DH)
    base = jax.random.normal(random_key_root, shape, jnp.float32)
    query_scale = jnp.exp(jax.random.uniform(random_key_queryscale, (SECTION_COUNT, SEQUENCE_COUNT, SEGMENT_TOKENS, H, 1), jnp.float32, math.log(0.2), math.log(2.0)))
    queries = base[:, :, :, :H, :] * query_scale
    key_part = base[:, :, :, H:H + KEY_VALUE_HEADS, :]
    value_part = base[:, :, :, H + KEY_VALUE_HEADS:, :]
    joined = jnp.concatenate([queries, key_part, value_part], axis=3)
    joined = jnp.clip(joined, -5.0, 5.0)
    return joined.reshape(SECTION_COUNT, SEQUENCE_COUNT, SEGMENT_TOKENS, (H + 2 * KEY_VALUE_HEADS) * DH).astype(jnp.bfloat16)


def steps_of(rng, dims, shards, least, largest):
    def one(dim, blocks):
        steps = jax.random.uniform(jax.random.fold_in(jax.random.fold_in(rng, 6), dim), (blocks,), jnp.float32, least / len(shards), largest / len(shards))
        return jnp.repeat(jnp.exp(steps), dims[dim] // blocks).reshape((-1,) + (1,) * (len(dims) - dim - 1))

    loudness = one(*shards[0])
    for cut in shards[1:]:
        loudness = loudness * one(*cut)
    return loudness


def gaussian(rng, dims, deviation, limit, cuts=(), kind=jnp.bfloat16):
    values = deviation * jax.random.normal(rng, dims, jnp.float32)
    if cuts:
        values = values * steps_of(rng, dims, cuts, -0.22, 0.18)
    return jnp.clip(values, -limit, limit).astype(kind)


def setup_inputs(seed: int = 0) -> dict:
    streams_of = jax.random.split(jax.random.key(seed), 6)
    return {
        "qkv_rows": draw_qkv_rows(jax.random.fold_in(streams_of[5], 71), 0),
        "grad_output": gaussian(streams_of[1], (SECTION_COUNT, SEQUENCE_COUNT, SEGMENT_TOKENS, H * DH), 2.0, 12.0, ((0, 8), (1, 64))),
        "memory_rows": gaussian(streams_of[2], (SECTION_COUNT, MEMBLOCKS, BLK, 2 * KEY_VALUE_HEADS * DH), 1.0, 5.0, ((0, 8), (1, 32))),
        "shard_fill": draw_shard_fill(jax.random.fold_in(streams_of[5], 71), 0),
        "block_ids": draw_block_ids(jax.random.fold_in(streams_of[5], 71), 0),
    }


NEG_FILL = -1e30


def rounded(values_in):
    return lax.optimization_barrier(values_in.astype(jnp.bfloat16)).astype(jnp.float32)


def sequence_pass(qkv_seq, grad_seq, ids_seq, memory_section, fill_section):
    groups = H // KEY_VALUE_HEADS
    inv_root = DH ** -0.5
    memory_len = TOPK * BLK
    width = KEY_VALUE_HEADS * DH
    queries = qkv_seq[:, :H * DH].astype(jnp.float32).reshape(QB, BLK, KEY_VALUE_HEADS, groups, DH)
    keys_local = qkv_seq[:, H * DH:(H + KEY_VALUE_HEADS) * DH].astype(jnp.float32).reshape(SEGMENT_TOKENS, KEY_VALUE_HEADS, DH)
    values_local = qkv_seq[:, (H + KEY_VALUE_HEADS) * DH:].astype(jnp.float32).reshape(SEGMENT_TOKENS, KEY_VALUE_HEADS, DH)
    flat_ids = ids_seq.reshape(-1).astype(jnp.int32)
    blocks = jnp.take(memory_section, flat_ids, axis=0).astype(jnp.float32).reshape(QB, memory_len, 2 * width)
    mem_keys = blocks[..., :width].reshape(QB, memory_len, KEY_VALUE_HEADS, DH)
    mem_values = blocks[..., width:].reshape(QB, memory_len, KEY_VALUE_HEADS, DH)
    key_rows = jnp.concatenate([mem_keys, jnp.broadcast_to(keys_local[None], (QB, SEGMENT_TOKENS, KEY_VALUE_HEADS, DH))], axis=1)
    value_rows = jnp.concatenate([mem_values, jnp.broadcast_to(values_local[None], (QB, SEGMENT_TOKENS, KEY_VALUE_HEADS, DH))], axis=1)
    owner_shard = (ids_seq // MB_DEV).astype(jnp.int32)
    slot_index = (ids_seq % MB_DEV).astype(jnp.int32)
    position = slot_index[:, :, None] * BLK + jnp.arange(BLK, dtype=jnp.int32)[None, None, :]
    live_mask = (position < jnp.take(fill_section, owner_shard)[:, :, None]).reshape(QB, memory_len)
    row_pos = jnp.arange(QB, dtype=jnp.int32)[:, None] * BLK + jnp.arange(BLK, dtype=jnp.int32)[None, :]
    causal = jnp.arange(SEGMENT_TOKENS, dtype=jnp.int32)[None, None, :] <= row_pos[:, :, None]
    key_mask = jnp.concatenate([jnp.broadcast_to(live_mask[:, None, :], (QB, BLK, memory_len)), causal], axis=-1)
    scores = jnp.einsum('bikhd,bnkd->bikhn', queries, key_rows) * inv_root
    scores = jnp.where(key_mask[:, :, None, None, :], scores, NEG_FILL)
    row_max = jnp.max(scores, axis=-1, keepdims=True)
    log_total = row_max + jnp.log(jnp.sum(jnp.exp(scores - row_max), axis=-1, keepdims=True))
    weights = jnp.exp(scores - log_total)
    prob_bf = rounded(weights)
    attended = rounded(jnp.einsum('bikhn,bnkd->bikhd', prob_bf, value_rows))
    grad_rows = grad_seq.astype(jnp.float32).reshape(QB, BLK, KEY_VALUE_HEADS, groups, DH)
    dprobs = jnp.einsum('bikhd,bnkd->bikhn', grad_rows, value_rows)
    row_delta = jnp.sum(grad_rows * attended, axis=-1, keepdims=True)
    dscores = rounded(weights * (dprobs - row_delta))
    grad_query = jnp.einsum('bikhn,bnkd->bikhd', dscores, key_rows) * inv_root
    grad_key = jnp.einsum('bikhn,bikhd->bnkd', dscores, queries) * inv_root
    grad_value = jnp.einsum('bikhn,bikhd->bnkd', prob_bf, grad_rows)
    local_key = jnp.sum(grad_key[:, memory_len:], axis=0).reshape(SEGMENT_TOKENS, width)
    local_value = jnp.sum(grad_value[:, memory_len:], axis=0).reshape(SEGMENT_TOKENS, width)
    seq_grads = jnp.concatenate([grad_query.reshape(SEGMENT_TOKENS, H * DH), local_key, local_value], axis=-1).astype(jnp.bfloat16)
    mem_key_grad = grad_key[:, :memory_len].reshape(QB * TOPK, BLK, width)
    mem_value_grad = grad_value[:, :memory_len].reshape(QB * TOPK, BLK, width)
    mem_part = jnp.concatenate([mem_key_grad, mem_value_grad], axis=-1).reshape(QB * TOPK, BLK * 2 * width)
    same_block = flat_ids[:, None] == flat_ids[None, :]
    combined = jnp.dot(same_block.astype(jnp.float32), mem_part, precision=lax.Precision.HIGHEST)
    entry_index = jnp.arange(QB * TOPK, dtype=jnp.int32)
    earlier = same_block & (entry_index[None, :] < entry_index[:, None])
    first_hit = jnp.logical_not(jnp.any(earlier, axis=1))
    contribution = jnp.where(first_hit[:, None], rounded(combined), jnp.float32(0.0))
    return seq_grads, flat_ids, contribution.reshape(QB * TOPK, BLK, 2 * width)


def section_pass(pieces):
    qkv_section, grad_section, ids_section, memory_section, fill_section = pieces

    def add_sequence(accum, sequence):
        qkv_seq, grad_seq, ids_seq = sequence
        seq_grads, flat_ids, contribution = sequence_pass(qkv_seq, grad_seq, ids_seq, memory_section, fill_section)
        return accum.at[flat_ids].add(contribution), seq_grads

    start = jnp.zeros((MEMBLOCKS, BLK, 2 * KEY_VALUE_HEADS * DH), jnp.float32)
    accum, section_grads = lax.scan(add_sequence, start, (qkv_section, grad_section, ids_section))
    return section_grads, accum.astype(jnp.bfloat16)


def reference(qkv_rows, grad_output, memory_rows, shard_fill, block_ids):
    section_grads, memory_grad = lax.map(section_pass, (qkv_rows, grad_output, block_ids, memory_rows, shard_fill))
    upstream = jnp.concatenate([section_grads[1:], jnp.zeros_like(section_grads[:1])], axis=0)
    return upstream, memory_grad
```

```python
from functools import partial

import jax
import jax.numpy as jnp
from jax import lax
from jax.sharding import PartitionSpec as P

H = 16
KEY_VALUE_HEADS = 4
DH = 128
BLK = 64


NEG_FILL = -1e30


def passed_along(array, axis, by):
    devices = lax.axis_size(axis)
    pairs = [(i, i + by) for i in range(devices) if 0 <= i + by < devices]
    return lax.ppermute(array, axis, pairs)


def head_scores(key_mask, queries, key_rows):
    raw = jnp.einsum(
        "bihd,bnd->bihn", queries, key_rows, preferred_element_type=jnp.float32
    ) * DH ** (-0.5)
    return jnp.where(key_mask[:, :, None, :], raw, NEG_FILL)


def head_forward(key_mask, pieces):
    queries, key_rows, value_rows = pieces
    scores = head_scores(key_mask, queries, key_rows)
    row_max = jnp.max(scores, axis=-1, keepdims=True)
    log_total = row_max + jnp.log(jnp.sum(jnp.exp(scores - row_max), axis=-1, keepdims=True))
    prob_bf = jnp.exp(scores - log_total).astype(jnp.bfloat16)
    attended = jnp.einsum(
        "bihn,bnd->bihd", prob_bf, value_rows, preferred_element_type=jnp.float32
    ).astype(jnp.bfloat16)
    return (log_total, attended)


def head_backward(key_mask, pieces):
    queries, key_rows, value_rows, grad_rows, log_total, attended = pieces
    scores = head_scores(key_mask, queries, key_rows)
    weights = jnp.exp(scores - log_total)
    prob_bf = weights.astype(jnp.bfloat16)
    dprobs = jnp.einsum("bihd,bnd->bihn", grad_rows, value_rows, preferred_element_type=jnp.float32)
    row_delta = jnp.sum(
        grad_rows.astype(jnp.float32) * attended.astype(jnp.float32), axis=-1, keepdims=True
    )
    dscores = (weights * (dprobs - row_delta)).astype(jnp.bfloat16)
    inv_root = DH ** (-0.5)
    grad_query = (
        jnp.einsum("bihn,bnd->bihd", dscores, key_rows, preferred_element_type=jnp.float32)
        * inv_root
    )
    grad_key = (
        jnp.einsum("bihn,bihd->bnd", dscores, queries, preferred_element_type=jnp.float32)
        * inv_root
    )
    grad_value = jnp.einsum(
        "bihn,bihd->bnd", prob_bf, grad_rows, preferred_element_type=jnp.float32
    )
    return (grad_query, grad_key, grad_value)


def assemble(slots, slot_live, owner_shard, keys_local, values_local):
    qblocks, topk = owner_shard.shape
    tokens = keys_local.shape[0]
    width = KEY_VALUE_HEADS * DH
    memory_len = topk * BLK
    picked = jnp.take(slots, owner_shard.reshape(-1), axis=0)
    mem_keys = picked[..., :width].reshape(qblocks, memory_len, KEY_VALUE_HEADS, DH)
    mem_values = picked[..., width:].reshape(qblocks, memory_len, KEY_VALUE_HEADS, DH)
    key_rows = jnp.concatenate(
        [mem_keys, jnp.broadcast_to(keys_local[None], (qblocks, tokens, KEY_VALUE_HEADS, DH))],
        axis=1,
    )
    value_rows = jnp.concatenate(
        [mem_values, jnp.broadcast_to(values_local[None], (qblocks, tokens, KEY_VALUE_HEADS, DH))],
        axis=1,
    )
    live_len = jnp.take(slot_live[:, 0], owner_shard.reshape(-1))
    live_mask = (jnp.arange(BLK)[None, :] < live_len[:, None]).reshape(qblocks, memory_len)
    row_pos = jnp.arange(qblocks)[:, None] * BLK + jnp.arange(BLK)[None, :]
    causal = jnp.arange(tokens)[None, None, :] <= row_pos[:, :, None]
    key_mask = jnp.concatenate(
        [jnp.broadcast_to(live_mask[:, None, :], (qblocks, BLK, memory_len)), causal], axis=-1
    )
    return (
        jnp.transpose(key_rows, (2, 0, 1, 3)),
        jnp.transpose(value_rows, (2, 0, 1, 3)),
        key_mask,
    )


def per_device(qkv_rows, grad_output, memory_rows, shard_fill, block_ids):
    shards = lax.axis_size("mem")
    groups = H // KEY_VALUE_HEADS
    width = KEY_VALUE_HEADS * DH
    rows_here = qkv_rows[0, 0]
    tokens = rows_here.shape[0]
    ids_here = block_ids[0, 0]
    qblocks, topk = ids_here.shape
    memory_len = topk * BLK
    held_blocks = memory_rows.shape[1]
    queries = rows_here[:, : H * DH].reshape(qblocks, BLK, KEY_VALUE_HEADS, groups, DH)
    keys_local = rows_here[:, H * DH : (H + KEY_VALUE_HEADS) * DH].reshape(
        tokens, KEY_VALUE_HEADS, DH
    )
    values_local = rows_here[:, (H + KEY_VALUE_HEADS) * DH :].reshape(tokens, KEY_VALUE_HEADS, DH)
    grad_rows = grad_output[0, 0].reshape(qblocks, BLK, KEY_VALUE_HEADS, groups, DH)
    queries_head = jnp.transpose(queries, (2, 0, 1, 3, 4))
    grads_head = jnp.transpose(grad_rows, (2, 0, 1, 3, 4))
    owner_shard = ids_here // held_blocks
    slot_index = ids_here % held_blocks
    shard_ids = jnp.arange(shards, dtype=jnp.int32)
    hits = owner_shard[:, :, None] == shard_ids[None, None, :]
    request = jnp.max(jnp.where(hits, slot_index[:, :, None], -1), axis=(0, 1))
    wanted = lax.all_to_all(request[:, None], "mem", split_axis=0, concat_axis=0, tiled=True)[:, 0]
    picked = jnp.take(memory_rows[0], jnp.maximum(wanted, 0), axis=0)
    fills = lax.all_gather(shard_fill[0, 0], "mem")
    slot_live = jnp.where(request >= 0, jnp.clip(fills - request * BLK, 0, BLK), 0)[:, None]
    slots = lax.all_to_all(picked, "mem", split_axis=0, concat_axis=0, tiled=True)
    key_rows, value_rows, key_mask = assemble(
        slots, slot_live, owner_shard, keys_local, values_local
    )
    log_total, attended = lax.map(
        partial(head_forward, key_mask), (queries_head, key_rows, value_rows)
    )
    grad_query, grad_key, grad_value = lax.map(
        partial(head_backward, key_mask),
        (queries_head, key_rows, value_rows, grads_head, log_total, attended),
    )
    query_part = jnp.transpose(grad_query, (1, 2, 0, 3, 4)).reshape(tokens, H * DH)
    local_key = jnp.transpose(jnp.sum(grad_key[:, :, memory_len:], axis=1), (1, 0, 2)).reshape(
        tokens, width
    )
    local_value = jnp.transpose(jnp.sum(grad_value[:, :, memory_len:], axis=1), (1, 0, 2)).reshape(
        tokens, width
    )
    section_grads = jnp.concatenate([query_part, local_key, local_value], axis=-1).astype(
        jnp.bfloat16
    )
    upstream = passed_along(section_grads[None, None], "section", -1)
    mem_key_grad = jnp.transpose(grad_key[:, :, :memory_len], (1, 2, 0, 3)).reshape(
        qblocks, topk, BLK * width
    )
    mem_value_grad = jnp.transpose(grad_value[:, :, :memory_len], (1, 2, 0, 3)).reshape(
        qblocks, topk, BLK * width
    )
    key_slot = jnp.sum(jnp.where(hits, jnp.arange(topk, dtype=jnp.int32)[None, :, None], 0), axis=1)
    present = jnp.any(hits, axis=1)[:, :, None, None]
    entry_grads = jnp.concatenate(
        [
            mem_key_grad.reshape(qblocks, topk, BLK, width),
            mem_value_grad.reshape(qblocks, topk, BLK, width),
        ],
        axis=-1,
    )
    placed = jnp.take_along_axis(entry_grads, key_slot[:, :, None, None], axis=1)
    slot_grads = jnp.sum(jnp.where(present, placed, jnp.float32(0.0)), axis=0).astype(jnp.bfloat16)
    received = lax.all_to_all(slot_grads, "mem", split_axis=0, concat_axis=0, tiled=True)
    wanted_hot = (wanted[:, None] == jnp.arange(held_blocks, dtype=jnp.int32)[None, :]).astype(
        jnp.bfloat16
    )
    owned = jnp.einsum(
        "rj,rx->jx",
        wanted_hot,
        received.reshape(shards, BLK * 2 * width),
        preferred_element_type=jnp.float32,
    )
    summed = lax.psum(owned, "dp")
    memory_grad = summed.astype(jnp.bfloat16).reshape(1, held_blocks, BLK, 2 * width)
    return (upstream, memory_grad)


def solution(mesh):
    placed = (
        P("section", ("dp", "mem"), None, None),
        P("section", ("dp", "mem"), None, None),
        P("section", "mem", None, None),
        P("section", "mem"),
        P("section", ("dp", "mem"), None, None),
    )
    return jax.shard_map(
        per_device,
        mesh=mesh,
        in_specs=placed,
        out_specs=(P("section", ("dp", "mem"), None, None), P("section", "mem", None, None)),
        check_vma=False,
    )
```

```python
from functools import partial

import jax
import jax.numpy as jnp
from jax import lax
from jax.sharding import PartitionSpec as P

H = 16
KEY_VALUE_HEADS = 4
DH = 128
BLK = 64


NEG_FILL = -1e30


def passed_along(array, axis, by):
    devices = lax.axis_size(axis)
    pairs = [(i, i + by) for i in range(devices) if 0 <= i + by < devices]
    return lax.ppermute(array, axis, pairs)


def head_scores(key_mask, queries, key_rows):
    raw = jnp.einsum(
        "bihd,bnd->bihn", queries, key_rows, preferred_element_type=jnp.float32
    ) * DH ** (-0.5)
    return jnp.where(key_mask[:, :, None, :], raw, NEG_FILL)


def head_forward(key_mask, pieces):
    queries, key_rows, value_rows = pieces
    scores = head_scores(key_mask, queries, key_rows)
    row_max = jnp.max(scores, axis=-1, keepdims=True)
    log_total = row_max + jnp.log(jnp.sum(jnp.exp(scores - row_max), axis=-1, keepdims=True))
    prob_bf = jnp.exp(scores - log_total).astype(jnp.bfloat16)
    attended = jnp.einsum(
        "bihn,bnd->bihd", prob_bf, value_rows, preferred_element_type=jnp.float32
    ).astype(jnp.bfloat16)
    return (log_total, attended)


def head_backward(key_mask, pieces):
    queries, key_rows, value_rows, grad_rows, log_total, attended = pieces
    scores = head_scores(key_mask, queries, key_rows)
    weights = jnp.exp(scores - log_total)
    prob_bf = weights.astype(jnp.bfloat16)
    dprobs = jnp.einsum("bihd,bnd->bihn", grad_rows, value_rows, preferred_element_type=jnp.float32)
    row_delta = jnp.sum(
        grad_rows.astype(jnp.float32) * attended.astype(jnp.float32), axis=-1, keepdims=True
    )
    dscores = (weights * (dprobs - row_delta)).astype(jnp.bfloat16)
    inv_root = DH ** (-0.5)
    grad_query = (
        jnp.einsum("bihn,bnd->bihd", dscores, key_rows, preferred_element_type=jnp.float32)
        * inv_root
    )
    grad_key = (
        jnp.einsum("bihn,bihd->bnd", dscores, queries, preferred_element_type=jnp.float32)
        * inv_root
    )
    grad_value = jnp.einsum(
        "bihn,bihd->bnd", prob_bf, grad_rows, preferred_element_type=jnp.float32
    )
    return (grad_query, grad_key, grad_value)


def assemble(slots_head, slot_live, owner_shard, keys_local, values_local):
    qblocks, topk = owner_shard.shape
    tokens = keys_local.shape[0]
    memory_len = topk * BLK
    picked = jnp.take(slots_head, owner_shard.reshape(-1), axis=0)
    mem_keys = picked[:, :, 0].reshape(qblocks, memory_len, DH)
    mem_values = picked[:, :, 1].reshape(qblocks, memory_len, DH)
    key_rows = jnp.concatenate(
        [mem_keys, jnp.broadcast_to(keys_local[None], (qblocks, tokens, DH))], axis=1
    )
    value_rows = jnp.concatenate(
        [mem_values, jnp.broadcast_to(values_local[None], (qblocks, tokens, DH))], axis=1
    )
    live_len = jnp.take(slot_live, owner_shard.reshape(-1))
    live_mask = (jnp.arange(BLK)[None, :] < live_len[:, None]).reshape(qblocks, memory_len)
    row_pos = jnp.arange(qblocks)[:, None] * BLK + jnp.arange(BLK)[None, :]
    causal = jnp.arange(tokens)[None, None, :] <= row_pos[:, :, None]
    key_mask = jnp.concatenate(
        [jnp.broadcast_to(live_mask[:, None, :], (qblocks, BLK, memory_len)), causal], axis=-1
    )
    return key_rows, value_rows, key_mask


def per_device(qkv_rows, grad_output, memory_rows, shard_fill, block_ids):
    shards = lax.axis_size("mem")
    groups = H // KEY_VALUE_HEADS
    rows_here = qkv_rows[0, 0]
    tokens = rows_here.shape[0]
    ids_here = block_ids[0, 0]
    qblocks, topk = ids_here.shape
    memory_len = topk * BLK
    held_blocks = memory_rows.shape[1]
    queries = rows_here[:, : H * DH].reshape(qblocks, BLK, KEY_VALUE_HEADS, groups, DH)
    keys_local = rows_here[:, H * DH : (H + KEY_VALUE_HEADS) * DH].reshape(
        tokens, KEY_VALUE_HEADS, DH
    )
    values_local = rows_here[:, (H + KEY_VALUE_HEADS) * DH :].reshape(tokens, KEY_VALUE_HEADS, DH)
    grad_rows = grad_output[0, 0].reshape(qblocks, BLK, KEY_VALUE_HEADS, groups, DH)
    owner_shard = ids_here // held_blocks
    slot_index = ids_here % held_blocks
    shard_ids = jnp.arange(shards, dtype=jnp.int32)
    hits = owner_shard[:, :, None] == shard_ids[None, None, :]
    request = jnp.max(jnp.where(hits, slot_index[:, :, None], -1), axis=(0, 1))
    shared = jnp.concatenate([ids_here.reshape(-1), shard_fill[0, 0].reshape(1)])
    gathered = lax.all_gather(shared, "mem")
    peer_ids = gathered[:, : qblocks * topk]
    fills = gathered[:, qblocks * topk]
    mine = lax.axis_index("mem")
    wanted = jnp.max(
        jnp.where(peer_ids // held_blocks == mine, peer_ids % held_blocks, -1), axis=1
    )
    slot_live = jnp.where(request >= 0, jnp.clip(fills - request * BLK, 0, BLK), 0)
    picked = jnp.take(memory_rows[0], jnp.maximum(wanted, 0), axis=0).reshape(
        shards, BLK, 2, KEY_VALUE_HEADS, DH
    )
    key_slot = jnp.sum(jnp.where(hits, jnp.arange(topk, dtype=jnp.int32)[None, :, None], 0), axis=1)
    present = jnp.any(hits, axis=1)[:, :, None, None, None]
    wanted_hot = (wanted[:, None] == jnp.arange(held_blocks, dtype=jnp.int32)[None, :]).astype(
        jnp.bfloat16
    )
    upstream_parts = []
    owned_parts = []
    payloads = [picked[:, :, :, head] for head in range(KEY_VALUE_HEADS)]
    sent_grads = []
    for head in range(KEY_VALUE_HEADS):
        payload = payloads[head]
        if head >= 2:
            payload, sent_grads[head - 2] = lax.optimization_barrier(
                (payload, sent_grads[head - 2])
            )
        slots_head = lax.all_to_all(payload, "mem", split_axis=0, concat_axis=0, tiled=True)
        key_rows, value_rows, key_mask = assemble(
            slots_head, slot_live, owner_shard, keys_local[:, head], values_local[:, head]
        )
        queries_head = queries[:, :, head]
        grads_head = grad_rows[:, :, head]
        log_total, attended = head_forward(key_mask, (queries_head, key_rows, value_rows))
        grad_query, grad_key, grad_value = head_backward(
            key_mask,
            (queries_head, key_rows, value_rows, grads_head, log_total, attended),
        )
        upstream_parts.append(
            jnp.concatenate(
                [
                    grad_query.reshape(tokens, groups * DH),
                    jnp.sum(grad_key[:, memory_len:], axis=0),
                    jnp.sum(grad_value[:, memory_len:], axis=0),
                ],
                axis=-1,
            ).astype(jnp.bfloat16)
        )
        entry_grads = jnp.stack(
            [
                grad_key[:, :memory_len].reshape(qblocks, topk, BLK, DH),
                grad_value[:, :memory_len].reshape(qblocks, topk, BLK, DH),
            ],
            axis=3,
        )
        placed = jnp.take_along_axis(entry_grads, key_slot[:, :, None, None, None], axis=1)
        slot_grads = jnp.sum(jnp.where(present, placed, jnp.float32(0.0)), axis=0).astype(
            jnp.bfloat16
        )
        sent_grads.append(slot_grads)
    for head in range(KEY_VALUE_HEADS):
        received = lax.all_to_all(
            sent_grads[head], "mem", split_axis=0, concat_axis=0, tiled=True
        )
        owned = jnp.einsum(
            "rj,rx->jx",
            wanted_hot,
            received.reshape(shards, BLK * 2 * DH),
            preferred_element_type=jnp.float32,
        )
        owned_parts.append(lax.psum(owned, "dp").reshape(held_blocks, BLK, 2, DH))
    moved = [passed_along(part, "section", -1) for part in upstream_parts]
    width_q = groups * DH
    upstream = jnp.concatenate(
        [part[:, :width_q] for part in moved]
        + [part[:, width_q : width_q + DH] for part in moved]
        + [part[:, width_q + DH :] for part in moved],
        axis=-1,
    )
    summed = jnp.stack(owned_parts, axis=3)
    memory_grad = summed.astype(jnp.bfloat16).reshape(1, held_blocks, BLK, 2 * KEY_VALUE_HEADS * DH)
    return (upstream[None, None], memory_grad)


def solution(mesh):
    placed = (
        P("section", ("dp", "mem"), None, None),
        P("section", ("dp", "mem"), None, None),
        P("section", "mem", None, None),
        P("section", "mem"),
        P("section", ("dp", "mem"), None, None),
    )
    return jax.shard_map(
        per_device,
        mesh=mesh,
        in_specs=placed,
        out_specs=(P("section", ("dp", "mem"), None, None), P("section", "mem", None, None)),
        check_vma=False,
    )
```

```python
from functools import partial

import jax
import jax.numpy as jnp
from jax import lax
from jax.sharding import PartitionSpec as P

H = 16
KEY_VALUE_HEADS = 4
DH = 128
BLK = 64


NEG_FILL = -1e30


def passed_along(array, axis, by):
    devices = lax.axis_size(axis)
    pairs = [(i, i + by) for i in range(devices) if 0 <= i + by < devices]
    return lax.ppermute(array, axis, pairs)


def head_scores(key_mask, queries, key_rows):
    raw = jnp.einsum(
        "bihd,bnd->bihn", queries, key_rows, preferred_element_type=jnp.float32
    ) * DH ** (-0.5)
    return jnp.where(key_mask[:, :, None, :], raw, NEG_FILL)


def head_forward(key_mask, pieces):
    queries, key_rows, value_rows = pieces
    scores = head_scores(key_mask, queries, key_rows)
    row_max = jnp.max(scores, axis=-1, keepdims=True)
    log_total = row_max + jnp.log(jnp.sum(jnp.exp(scores - row_max), axis=-1, keepdims=True))
    prob_bf = jnp.exp(scores - log_total).astype(jnp.bfloat16)
    attended = jnp.einsum(
        "bihn,bnd->bihd", prob_bf, value_rows, preferred_element_type=jnp.float32
    ).astype(jnp.bfloat16)
    return (log_total, attended)


def head_backward(key_mask, pieces):
    queries, key_rows, value_rows, grad_rows, log_total, attended = pieces
    scores = head_scores(key_mask, queries, key_rows)
    weights = jnp.exp(scores - log_total)
    prob_bf = weights.astype(jnp.bfloat16)
    dprobs = jnp.einsum("bihd,bnd->bihn", grad_rows, value_rows, preferred_element_type=jnp.float32)
    row_delta = jnp.sum(
        grad_rows.astype(jnp.float32) * attended.astype(jnp.float32), axis=-1, keepdims=True
    )
    dscores = (weights * (dprobs - row_delta)).astype(jnp.bfloat16)
    inv_root = DH ** (-0.5)
    grad_query = (
        jnp.einsum("bihn,bnd->bihd", dscores, key_rows, preferred_element_type=jnp.float32)
        * inv_root
    )
    grad_key = (
        jnp.einsum("bihn,bihd->bnd", dscores, queries, preferred_element_type=jnp.float32)
        * inv_root
    )
    grad_value = jnp.einsum(
        "bihn,bihd->bnd", prob_bf, grad_rows, preferred_element_type=jnp.float32
    )
    return (grad_query, grad_key, grad_value)


def masks(slot_live, owner_shard, tokens):
    qblocks, topk = owner_shard.shape
    memory_len = topk * BLK
    live_len = jnp.take(slot_live, owner_shard.reshape(-1))
    live_mask = (jnp.arange(BLK)[None, :] < live_len[:, None]).reshape(qblocks, memory_len)
    row_pos = jnp.arange(qblocks)[:, None] * BLK + jnp.arange(BLK)[None, :]
    causal = jnp.arange(tokens)[None, None, :] <= row_pos[:, :, None]
    return jnp.concatenate(
        [jnp.broadcast_to(live_mask[:, None, :], (qblocks, BLK, memory_len)), causal], axis=-1
    )


def per_device(qkv_rows, grad_output, memory_rows, shard_fill, block_ids):
    shards = lax.axis_size("mem")
    groups = H // KEY_VALUE_HEADS
    rows_here = qkv_rows[0, 0]
    tokens = rows_here.shape[0]
    ids_here = block_ids[0, 0]
    qblocks, topk = ids_here.shape
    memory_len = topk * BLK
    held_blocks = memory_rows.shape[1]
    queries = rows_here[:, : H * DH].reshape(qblocks, BLK, KEY_VALUE_HEADS, groups, DH)
    keys_local = rows_here[:, H * DH : (H + KEY_VALUE_HEADS) * DH].reshape(
        tokens, KEY_VALUE_HEADS, DH
    )
    values_local = rows_here[:, (H + KEY_VALUE_HEADS) * DH :].reshape(tokens, KEY_VALUE_HEADS, DH)
    grad_rows = grad_output[0, 0].reshape(qblocks, BLK, KEY_VALUE_HEADS, groups, DH)
    owner_shard = ids_here // held_blocks
    slot_index = ids_here % held_blocks
    shard_ids = jnp.arange(shards, dtype=jnp.int32)
    hits = owner_shard[:, :, None] == shard_ids[None, None, :]
    request = jnp.max(jnp.where(hits, slot_index[:, :, None], -1), axis=(0, 1))
    shared = jnp.concatenate([ids_here.reshape(-1), shard_fill[0, 0].reshape(1)])
    gathered = lax.all_gather(shared, "mem")
    peer_ids = gathered[:, : qblocks * topk]
    fills = gathered[:, qblocks * topk]
    mine = lax.axis_index("mem")
    wanted = jnp.max(
        jnp.where(peer_ids // held_blocks == mine, peer_ids % held_blocks, -1), axis=1
    )
    slot_live = jnp.where(request >= 0, jnp.clip(fills - request * BLK, 0, BLK), 0)
    key_mask = masks(slot_live, owner_shard, tokens)
    memory_5d = memory_rows[0].reshape(held_blocks, BLK, 2, KEY_VALUE_HEADS, DH)
    wanted_hot = (wanted[:, None] == jnp.arange(held_blocks, dtype=jnp.int32)[None, :]).astype(
        jnp.bfloat16
    )
    entry_hot = (owner_shard.reshape(-1)[:, None] == shard_ids[None, :]).astype(jnp.bfloat16)
    per_chunk = 2
    chunks = KEY_VALUE_HEADS // per_chunk
    query_parts, key_parts, value_parts, owned_parts, sent_grads = [], [], [], [], []
    for chunk in range(chunks):
        first = chunk * per_chunk
        payload = jnp.einsum(
            "rj,jtkhd->rtkhd",
            wanted_hot,
            memory_5d[:, :, :, first : first + per_chunk],
            preferred_element_type=jnp.bfloat16,
        )
        if chunk >= 2:
            payload, sent_grads[chunk - 2] = lax.optimization_barrier(
                (payload, sent_grads[chunk - 2])
            )
        slots = lax.all_to_all(payload, "mem", split_axis=0, concat_axis=0, tiled=True)
        chosen = jnp.einsum(
            "es,stkhd->etkhd", entry_hot, slots, preferred_element_type=jnp.bfloat16
        )
        entries = []
        for inner in range(per_chunk):
            head = first + inner
            mem_keys = chosen[:, :, 0, inner].reshape(qblocks, memory_len, DH)
            mem_values = chosen[:, :, 1, inner].reshape(qblocks, memory_len, DH)
            key_rows = jnp.concatenate(
                [mem_keys, jnp.broadcast_to(keys_local[None, :, head], (qblocks, tokens, DH))],
                axis=1,
            )
            value_rows = jnp.concatenate(
                [mem_values, jnp.broadcast_to(values_local[None, :, head], (qblocks, tokens, DH))],
                axis=1,
            )
            queries_head = queries[:, :, head]
            grads_head = grad_rows[:, :, head]
            log_total, attended = head_forward(key_mask, (queries_head, key_rows, value_rows))
            grad_query, grad_key, grad_value = head_backward(
                key_mask,
                (queries_head, key_rows, value_rows, grads_head, log_total, attended),
            )
            query_parts.append(grad_query.reshape(tokens, groups * DH))
            key_parts.append(jnp.sum(grad_key[:, memory_len:], axis=0))
            value_parts.append(jnp.sum(grad_value[:, memory_len:], axis=0))
            entries.append(
                jnp.stack(
                    [
                        grad_key[:, :memory_len].reshape(qblocks * topk, BLK, DH),
                        grad_value[:, :memory_len].reshape(qblocks * topk, BLK, DH),
                    ],
                    axis=2,
                )
            )
        entry_grads = jnp.stack(entries, axis=3)
        slot_grads = jnp.einsum(
            "es,etkhd->stkhd",
            entry_hot.astype(jnp.float32),
            entry_grads,
            precision=lax.Precision.HIGHEST,
            preferred_element_type=jnp.float32,
        ).astype(jnp.bfloat16)
        sent_grads.append(slot_grads)
    for chunk in range(chunks):
        received = lax.all_to_all(
            sent_grads[chunk], "mem", split_axis=0, concat_axis=0, tiled=True
        )
        owned = jnp.einsum(
            "rj,rtkhd->jtkhd", wanted_hot, received, preferred_element_type=jnp.float32
        )
        owned_parts.append(lax.psum(owned, "dp"))
    section_grads = jnp.concatenate(query_parts + key_parts + value_parts, axis=-1).astype(
        jnp.bfloat16
    )
    upstream = passed_along(section_grads[None, None], "section", -1)
    summed = jnp.concatenate(owned_parts, axis=3)
    memory_grad = summed.astype(jnp.bfloat16).reshape(1, held_blocks, BLK, 2 * KEY_VALUE_HEADS * DH)
    return (upstream, memory_grad)


def solution(mesh):
    placed = (
        P("section", ("dp", "mem"), None, None),
        P("section", ("dp", "mem"), None, None),
        P("section", "mem", None, None),
        P("section", "mem"),
        P("section", ("dp", "mem"), None, None),
    )
    return jax.shard_map(
        per_device,
        mesh=mesh,
        in_specs=placed,
        out_specs=(P("section", ("dp", "mem"), None, None), P("section", "mem", None, None)),
        check_vma=False,
    )
```

```python
from functools import partial

import jax
import jax.numpy as jnp
from jax import lax
from jax.sharding import PartitionSpec as P

H = 16
KEY_VALUE_HEADS = 4
DH = 128
BLK = 64


NEG_FILL = -1e30


def passed_along(array, axis, by):
    devices = lax.axis_size(axis)
    pairs = [(i, i + by) for i in range(devices) if 0 <= i + by < devices]
    return lax.ppermute(array, axis, pairs)


def head_scores(key_mask, queries, key_rows):
    raw = jnp.einsum(
        "bihd,bnd->bihn", queries, key_rows, preferred_element_type=jnp.float32
    ) * DH ** (-0.5)
    return jnp.where(key_mask[:, :, None, :], raw, NEG_FILL)


def head_forward(key_mask, pieces):
    queries, key_rows, value_rows = pieces
    scores = head_scores(key_mask, queries, key_rows)
    row_max = jnp.max(scores, axis=-1, keepdims=True)
    log_total = row_max + jnp.log(jnp.sum(jnp.exp(scores - row_max), axis=-1, keepdims=True))
    prob_bf = jnp.exp(scores - log_total).astype(jnp.bfloat16)
    attended = jnp.einsum(
        "bihn,bnd->bihd", prob_bf, value_rows, preferred_element_type=jnp.float32
    ).astype(jnp.bfloat16)
    return (log_total, attended)


def head_backward(key_mask, pieces):
    queries, key_rows, value_rows, grad_rows, log_total, attended = pieces
    scores = head_scores(key_mask, queries, key_rows)
    weights = jnp.exp(scores - log_total)
    prob_bf = weights.astype(jnp.bfloat16)
    dprobs = jnp.einsum("bihd,bnd->bihn", grad_rows, value_rows, preferred_element_type=jnp.float32)
    row_delta = jnp.sum(
        grad_rows.astype(jnp.float32) * attended.astype(jnp.float32), axis=-1, keepdims=True
    )
    dscores = (weights * (dprobs - row_delta)).astype(jnp.bfloat16)
    inv_root = DH ** (-0.5)
    grad_query = (
        jnp.einsum("bihn,bnd->bihd", dscores, key_rows, preferred_element_type=jnp.float32)
        * inv_root
    )
    grad_key = (
        jnp.einsum("bihn,bihd->bnd", dscores, queries, preferred_element_type=jnp.float32)
        * inv_root
    )
    grad_value = jnp.einsum(
        "bihn,bihd->bnd", prob_bf, grad_rows, preferred_element_type=jnp.float32
    )
    return (grad_query, grad_key, grad_value)


def masks(slot_live, owner_shard, tokens):
    qblocks, topk = owner_shard.shape
    memory_len = topk * BLK
    live_len = jnp.take(slot_live, owner_shard.reshape(-1))
    live_mask = (jnp.arange(BLK)[None, :] < live_len[:, None]).reshape(qblocks, memory_len)
    row_pos = jnp.arange(qblocks)[:, None] * BLK + jnp.arange(BLK)[None, :]
    causal = jnp.arange(tokens)[None, None, :] <= row_pos[:, :, None]
    return jnp.concatenate(
        [jnp.broadcast_to(live_mask[:, None, :], (qblocks, BLK, memory_len)), causal], axis=-1
    )


def per_device(qkv_rows, grad_output, memory_rows, shard_fill, block_ids):
    shards = lax.axis_size("mem")
    groups = H // KEY_VALUE_HEADS
    rows_here = qkv_rows[0, 0]
    tokens = rows_here.shape[0]
    ids_here = block_ids[0, 0]
    qblocks, topk = ids_here.shape
    memory_len = topk * BLK
    held_blocks = memory_rows.shape[1]
    queries = rows_here[:, : H * DH].reshape(qblocks, BLK, KEY_VALUE_HEADS, groups, DH)
    keys_local = rows_here[:, H * DH : (H + KEY_VALUE_HEADS) * DH].reshape(
        tokens, KEY_VALUE_HEADS, DH
    )
    values_local = rows_here[:, (H + KEY_VALUE_HEADS) * DH :].reshape(tokens, KEY_VALUE_HEADS, DH)
    grad_rows = grad_output[0, 0].reshape(qblocks, BLK, KEY_VALUE_HEADS, groups, DH)
    owner_shard = ids_here // held_blocks
    slot_index = ids_here % held_blocks
    shard_ids = jnp.arange(shards, dtype=jnp.int32)
    hits = owner_shard[:, :, None] == shard_ids[None, None, :]
    request = jnp.max(jnp.where(hits, slot_index[:, :, None], -1), axis=(0, 1))
    shared = jnp.concatenate([ids_here.reshape(-1), shard_fill[0, 0].reshape(1)])
    gathered = lax.all_gather(shared, "mem")
    peer_ids = gathered[:, : qblocks * topk]
    fills = gathered[:, qblocks * topk]
    mine = lax.axis_index("mem")
    wanted = jnp.max(
        jnp.where(peer_ids // held_blocks == mine, peer_ids % held_blocks, -1), axis=1
    )
    slot_live = jnp.where(request >= 0, jnp.clip(fills - request * BLK, 0, BLK), 0)
    key_mask = masks(slot_live, owner_shard, tokens)
    memory_5d = memory_rows[0].reshape(held_blocks, BLK, 2, KEY_VALUE_HEADS, DH)
    wanted_hot = (wanted[:, None] == jnp.arange(held_blocks, dtype=jnp.int32)[None, :]).astype(
        jnp.bfloat16
    )
    entry_hot = (owner_shard.reshape(-1)[:, None] == shard_ids[None, :]).astype(jnp.bfloat16)
    per_chunk = 1
    chunks = KEY_VALUE_HEADS // per_chunk
    query_parts, key_parts, value_parts, owned_parts, sent_grads = [], [], [], [], []
    for chunk in range(chunks):
        first = chunk * per_chunk
        payload = jnp.einsum(
            "rj,jtkhd->rtkhd",
            wanted_hot,
            memory_5d[:, :, :, first : first + per_chunk],
            preferred_element_type=jnp.bfloat16,
        )
        if chunk >= 2:
            payload, sent_grads[chunk - 2] = lax.optimization_barrier(
                (payload, sent_grads[chunk - 2])
            )
        slots = lax.all_to_all(payload, "mem", split_axis=0, concat_axis=0, tiled=True)
        chosen = jnp.einsum(
            "es,stkhd->etkhd", entry_hot, slots, preferred_element_type=jnp.bfloat16
        )
        entries = []
        for inner in range(per_chunk):
            head = first + inner
            mem_keys = chosen[:, :, 0, inner].reshape(qblocks, memory_len, DH)
            mem_values = chosen[:, :, 1, inner].reshape(qblocks, memory_len, DH)
            key_rows = jnp.concatenate(
                [mem_keys, jnp.broadcast_to(keys_local[None, :, head], (qblocks, tokens, DH))],
                axis=1,
            )
            value_rows = jnp.concatenate(
                [mem_values, jnp.broadcast_to(values_local[None, :, head], (qblocks, tokens, DH))],
                axis=1,
            )
            queries_head = queries[:, :, head]
            grads_head = grad_rows[:, :, head]
            log_total, attended = head_forward(key_mask, (queries_head, key_rows, value_rows))
            grad_query, grad_key, grad_value = head_backward(
                key_mask,
                (queries_head, key_rows, value_rows, grads_head, log_total, attended),
            )
            query_parts.append(grad_query.reshape(tokens, groups * DH))
            key_parts.append(jnp.sum(grad_key[:, memory_len:], axis=0))
            value_parts.append(jnp.sum(grad_value[:, memory_len:], axis=0))
            entries.append(
                jnp.stack(
                    [
                        grad_key[:, :memory_len].reshape(qblocks * topk, BLK, DH),
                        grad_value[:, :memory_len].reshape(qblocks * topk, BLK, DH),
                    ],
                    axis=2,
                )
            )
        entry_grads = jnp.stack(entries, axis=3)
        slot_grads = jnp.einsum(
            "es,etkhd->stkhd",
            entry_hot.astype(jnp.float32),
            entry_grads,
            precision=lax.Precision.HIGHEST,
            preferred_element_type=jnp.float32,
        ).astype(jnp.bfloat16)
        sent_grads.append(slot_grads)
    for chunk in range(chunks):
        received = lax.all_to_all(
            sent_grads[chunk], "mem", split_axis=0, concat_axis=0, tiled=True
        )
        owned = jnp.einsum(
            "rj,rtkhd->jtkhd", wanted_hot, received, preferred_element_type=jnp.float32
        )
        owned_parts.append(lax.psum(owned, "dp"))
    section_grads = jnp.concatenate(query_parts + key_parts + value_parts, axis=-1).astype(
        jnp.bfloat16
    )
    upstream = passed_along(section_grads[None, None], "section", -1)
    summed = jnp.concatenate(owned_parts, axis=3)
    memory_grad = summed.astype(jnp.bfloat16).reshape(1, held_blocks, BLK, 2 * KEY_VALUE_HEADS * DH)
    return (upstream, memory_grad)


def solution(mesh):
    placed = (
        P("section", ("dp", "mem"), None, None),
        P("section", ("dp", "mem"), None, None),
        P("section", "mem", None, None),
        P("section", "mem"),
        P("section", ("dp", "mem"), None, None),
    )
    return jax.shard_map(
        per_device,
        mesh=mesh,
        in_specs=placed,
        out_specs=(P("section", ("dp", "mem"), None, None), P("section", "mem", None, None)),
        check_vma=False,
    )
```

```python
from functools import partial

import jax
import jax.numpy as jnp
from jax import lax
from jax.sharding import PartitionSpec as P

H = 16
KEY_VALUE_HEADS = 4
DH = 128
BLK = 64


NEG_FILL = -1e30


def passed_along(array, axis, by):
    devices = lax.axis_size(axis)
    pairs = [(i, i + by) for i in range(devices) if 0 <= i + by < devices]
    return lax.ppermute(array, axis, pairs)


def head_scores(key_mask, queries, key_rows):
    raw = jnp.einsum(
        "bighd,gbnd->bighn", queries, key_rows, preferred_element_type=jnp.float32
    ) * DH ** (-0.5)
    return jnp.where(key_mask[:, :, None, None, :], raw, NEG_FILL)


def head_forward(key_mask, pieces):
    queries, key_rows, value_rows = pieces
    scores = head_scores(key_mask, queries, key_rows)
    row_max = jnp.max(scores, axis=-1, keepdims=True)
    log_total = row_max + jnp.log(jnp.sum(jnp.exp(scores - row_max), axis=-1, keepdims=True))
    prob_bf = jnp.exp(scores - log_total).astype(jnp.bfloat16)
    attended = jnp.einsum(
        "bighn,gbnd->bighd", prob_bf, value_rows, preferred_element_type=jnp.float32
    ).astype(jnp.bfloat16)
    return (log_total, attended)


def head_backward(key_mask, pieces):
    queries, key_rows, value_rows, grad_rows, log_total, attended = pieces
    scores = head_scores(key_mask, queries, key_rows)
    weights = jnp.exp(scores - log_total)
    prob_bf = weights.astype(jnp.bfloat16)
    dprobs = jnp.einsum("bighd,gbnd->bighn", grad_rows, value_rows, preferred_element_type=jnp.float32)
    row_delta = jnp.sum(
        grad_rows.astype(jnp.float32) * attended.astype(jnp.float32), axis=-1, keepdims=True
    )
    dscores = (weights * (dprobs - row_delta)).astype(jnp.bfloat16)
    inv_root = DH ** (-0.5)
    grad_query = (
        jnp.einsum("bighn,gbnd->bighd", dscores, key_rows, preferred_element_type=jnp.float32)
        * inv_root
    )
    grad_key = (
        jnp.einsum("bighn,bighd->gbnd", dscores, queries, preferred_element_type=jnp.float32)
        * inv_root
    )
    grad_value = jnp.einsum(
        "bighn,bighd->gbnd", prob_bf, grad_rows, preferred_element_type=jnp.float32
    )
    return (grad_query, grad_key, grad_value)


def masks(slot_live, owner_shard, tokens):
    qblocks, topk = owner_shard.shape
    memory_len = topk * BLK
    live_len = jnp.take(slot_live, owner_shard.reshape(-1))
    live_mask = (jnp.arange(BLK)[None, :] < live_len[:, None]).reshape(qblocks, memory_len)
    row_pos = jnp.arange(qblocks)[:, None] * BLK + jnp.arange(BLK)[None, :]
    causal = jnp.arange(tokens)[None, None, :] <= row_pos[:, :, None]
    return jnp.concatenate(
        [jnp.broadcast_to(live_mask[:, None, :], (qblocks, BLK, memory_len)), causal], axis=-1
    )


def per_device(qkv_rows, grad_output, memory_rows, shard_fill, block_ids):
    shards = lax.axis_size("mem")
    groups = H // KEY_VALUE_HEADS
    rows_here = qkv_rows[0, 0]
    tokens = rows_here.shape[0]
    ids_here = block_ids[0, 0]
    qblocks, topk = ids_here.shape
    memory_len = topk * BLK
    held_blocks = memory_rows.shape[1]
    queries = rows_here[:, : H * DH].reshape(qblocks, BLK, KEY_VALUE_HEADS, groups, DH)
    keys_local = rows_here[:, H * DH : (H + KEY_VALUE_HEADS) * DH].reshape(
        tokens, KEY_VALUE_HEADS, DH
    )
    values_local = rows_here[:, (H + KEY_VALUE_HEADS) * DH :].reshape(tokens, KEY_VALUE_HEADS, DH)
    grad_rows = grad_output[0, 0].reshape(qblocks, BLK, KEY_VALUE_HEADS, groups, DH)
    owner_shard = ids_here // held_blocks
    slot_index = ids_here % held_blocks
    shard_ids = jnp.arange(shards, dtype=jnp.int32)
    hits = owner_shard[:, :, None] == shard_ids[None, None, :]
    request = jnp.max(jnp.where(hits, slot_index[:, :, None], -1), axis=(0, 1))
    shared = jnp.concatenate([ids_here.reshape(-1), shard_fill[0, 0].reshape(1)])
    gathered = lax.all_gather(shared, "mem")
    peer_ids = gathered[:, : qblocks * topk]
    fills = gathered[:, qblocks * topk]
    mine = lax.axis_index("mem")
    wanted = jnp.max(
        jnp.where(peer_ids // held_blocks == mine, peer_ids % held_blocks, -1), axis=1
    )
    slot_live = jnp.where(request >= 0, jnp.clip(fills - request * BLK, 0, BLK), 0)
    key_mask = masks(slot_live, owner_shard, tokens)
    memory_here = memory_rows[0]
    width = KEY_VALUE_HEADS * DH
    wanted_hot = (wanted[:, None] == jnp.arange(held_blocks, dtype=jnp.int32)[None, :]).astype(
        jnp.bfloat16
    )
    entry_hot = (owner_shard.reshape(-1)[:, None] == shard_ids[None, :]).astype(jnp.bfloat16)
    per_chunk = 2
    chunks = KEY_VALUE_HEADS // per_chunk
    span = per_chunk * DH
    query_parts, key_parts, value_parts, owned_parts, sent_grads = [], [], [], [], []
    for chunk in range(chunks):
        first = chunk * per_chunk
        lo = first * DH
        memory_chunk = jnp.concatenate(
            [memory_here[:, :, lo : lo + span], memory_here[:, :, width + lo : width + lo + span]],
            axis=-1,
        )
        payload = jnp.einsum(
            "rj,jtx->rtx", wanted_hot, memory_chunk, preferred_element_type=jnp.bfloat16
        )
        if chunk >= 2:
            payload, sent_grads[chunk - 2] = lax.optimization_barrier(
                (payload, sent_grads[chunk - 2])
            )
        slots = lax.all_to_all(payload, "mem", split_axis=0, concat_axis=0, tiled=True)
        chosen = jnp.einsum(
            "es,stx->etx", entry_hot, slots, preferred_element_type=jnp.bfloat16
        ).reshape(qblocks, memory_len, 2, per_chunk, DH)
        mem_keys = jnp.transpose(chosen[:, :, 0], (2, 0, 1, 3))
        mem_values = jnp.transpose(chosen[:, :, 1], (2, 0, 1, 3))
        local_keys = jnp.transpose(keys_local[:, first : first + per_chunk], (1, 0, 2))
        local_values = jnp.transpose(values_local[:, first : first + per_chunk], (1, 0, 2))
        key_rows = jnp.concatenate(
            [mem_keys, jnp.broadcast_to(local_keys[:, None], (per_chunk, qblocks, tokens, DH))],
            axis=2,
        )
        value_rows = jnp.concatenate(
            [mem_values, jnp.broadcast_to(local_values[:, None], (per_chunk, qblocks, tokens, DH))],
            axis=2,
        )
        queries_chunk = queries[:, :, first : first + per_chunk]
        grads_chunk = grad_rows[:, :, first : first + per_chunk]
        log_total, attended = head_forward(key_mask, (queries_chunk, key_rows, value_rows))
        grad_query, grad_key, grad_value = head_backward(
            key_mask,
            (queries_chunk, key_rows, value_rows, grads_chunk, log_total, attended),
        )
        query_parts.append(grad_query.reshape(tokens, per_chunk * groups * DH))
        key_parts.append(
            jnp.transpose(jnp.sum(grad_key[:, :, memory_len:], axis=1), (1, 0, 2)).reshape(
                tokens, span
            )
        )
        value_parts.append(
            jnp.transpose(jnp.sum(grad_value[:, :, memory_len:], axis=1), (1, 0, 2)).reshape(
                tokens, span
            )
        )
        entry_grads = jnp.stack(
            [grad_key[:, :, :memory_len], grad_value[:, :, :memory_len]], axis=0
        )
        entry_grads = jnp.transpose(
            entry_grads.reshape(2, per_chunk, qblocks * topk, BLK, DH), (2, 3, 0, 1, 4)
        ).reshape(qblocks * topk, BLK, 2 * span)
        slot_grads = jnp.einsum(
            "es,etx->stx",
            entry_hot.astype(jnp.float32),
            entry_grads,
            precision=lax.Precision.HIGHEST,
            preferred_element_type=jnp.float32,
        ).astype(jnp.bfloat16)
        sent_grads.append(slot_grads)
    for chunk in range(chunks):
        received = lax.all_to_all(
            sent_grads[chunk], "mem", split_axis=0, concat_axis=0, tiled=True
        )
        owned = jnp.einsum(
            "rj,rtx->jtx", wanted_hot, received, preferred_element_type=jnp.float32
        )
        owned_parts.append(lax.psum(owned, "dp"))
    section_grads = jnp.concatenate(query_parts + key_parts + value_parts, axis=-1).astype(
        jnp.bfloat16
    )
    upstream = passed_along(section_grads[None, None], "section", -1)
    summed = jnp.concatenate(
        [part[:, :, :span] for part in owned_parts] + [part[:, :, span:] for part in owned_parts],
        axis=-1,
    )
    memory_grad = summed.astype(jnp.bfloat16)[None]
    return (upstream, memory_grad)


def solution(mesh):
    placed = (
        P("section", ("dp", "mem"), None, None),
        P("section", ("dp", "mem"), None, None),
        P("section", "mem", None, None),
        P("section", "mem"),
        P("section", ("dp", "mem"), None, None),
    )
    return jax.shard_map(
        per_device,
        mesh=mesh,
        in_specs=placed,
        out_specs=(P("section", ("dp", "mem"), None, None), P("section", "mem", None, None)),
        check_vma=False,
    )
```

```python
from functools import partial

import jax
import jax.numpy as jnp
from jax import lax
from jax.sharding import PartitionSpec as P

H = 16
KEY_VALUE_HEADS = 4
DH = 128
BLK = 64


NEG_FILL = -1e30


def passed_along(array, axis, by):
    devices = lax.axis_size(axis)
    pairs = [(i, i + by) for i in range(devices) if 0 <= i + by < devices]
    return lax.ppermute(array, axis, pairs)


def head_scores(key_mask, queries, key_rows):
    raw = jnp.einsum(
        "bighd,gbnd->bighn", queries, key_rows, preferred_element_type=jnp.float32
    ) * DH ** (-0.5)
    return jnp.where(key_mask[:, :, None, None, :], raw, NEG_FILL)


def head_forward(key_mask, pieces):
    queries, key_rows, value_rows = pieces
    scores = head_scores(key_mask, queries, key_rows)
    row_max = jnp.max(scores, axis=-1, keepdims=True)
    log_total = row_max + jnp.log(jnp.sum(jnp.exp(scores - row_max), axis=-1, keepdims=True))
    prob_bf = jnp.exp(scores - log_total).astype(jnp.bfloat16)
    attended = jnp.einsum(
        "bighn,gbnd->bighd", prob_bf, value_rows, preferred_element_type=jnp.float32
    ).astype(jnp.bfloat16)
    return (log_total, attended)


def head_backward(key_mask, pieces):
    queries, key_rows, value_rows, grad_rows, log_total, attended = pieces
    scores = head_scores(key_mask, queries, key_rows)
    weights = jnp.exp(scores - log_total)
    prob_bf = weights.astype(jnp.bfloat16)
    dprobs = jnp.einsum("bighd,gbnd->bighn", grad_rows, value_rows, preferred_element_type=jnp.float32)
    row_delta = jnp.sum(
        grad_rows.astype(jnp.float32) * attended.astype(jnp.float32), axis=-1, keepdims=True
    )
    dscores = (weights * (dprobs - row_delta)).astype(jnp.bfloat16)
    inv_root = DH ** (-0.5)
    grad_query = (
        jnp.einsum("bighn,gbnd->bighd", dscores, key_rows, preferred_element_type=jnp.float32)
        * inv_root
    )
    grad_key = (
        jnp.einsum("bighn,bighd->gbnd", dscores, queries, preferred_element_type=jnp.float32)
        * inv_root
    )
    grad_value = jnp.einsum(
        "bighn,bighd->gbnd", prob_bf, grad_rows, preferred_element_type=jnp.float32
    )
    return (grad_query, grad_key, grad_value)


def masks(slot_live, owner_shard, tokens):
    qblocks, topk = owner_shard.shape
    memory_len = topk * BLK
    live_len = jnp.take(slot_live, owner_shard.reshape(-1))
    live_mask = (jnp.arange(BLK)[None, :] < live_len[:, None]).reshape(qblocks, memory_len)
    row_pos = jnp.arange(qblocks)[:, None] * BLK + jnp.arange(BLK)[None, :]
    causal = jnp.arange(tokens)[None, None, :] <= row_pos[:, :, None]
    return jnp.concatenate(
        [jnp.broadcast_to(live_mask[:, None, :], (qblocks, BLK, memory_len)), causal], axis=-1
    )


def per_device(qkv_rows, grad_output, memory_rows, shard_fill, block_ids):
    shards = lax.axis_size("mem")
    groups = H // KEY_VALUE_HEADS
    rows_here = qkv_rows[0, 0]
    tokens = rows_here.shape[0]
    ids_here = block_ids[0, 0]
    qblocks, topk = ids_here.shape
    memory_len = topk * BLK
    held_blocks = memory_rows.shape[1]
    queries = rows_here[:, : H * DH].reshape(qblocks, BLK, KEY_VALUE_HEADS, groups, DH)
    keys_local = rows_here[:, H * DH : (H + KEY_VALUE_HEADS) * DH].reshape(
        tokens, KEY_VALUE_HEADS, DH
    )
    values_local = rows_here[:, (H + KEY_VALUE_HEADS) * DH :].reshape(tokens, KEY_VALUE_HEADS, DH)
    grad_rows = grad_output[0, 0].reshape(qblocks, BLK, KEY_VALUE_HEADS, groups, DH)
    owner_shard = ids_here // held_blocks
    slot_index = ids_here % held_blocks
    shard_ids = jnp.arange(shards, dtype=jnp.int32)
    hits = owner_shard[:, :, None] == shard_ids[None, None, :]
    request = jnp.max(jnp.where(hits, slot_index[:, :, None], -1), axis=(0, 1))
    shared = jnp.concatenate([ids_here.reshape(-1), shard_fill[0, 0].reshape(1)])
    gathered = lax.all_gather(shared, "mem")
    peer_ids = gathered[:, : qblocks * topk]
    fills = gathered[:, qblocks * topk]
    mine = lax.axis_index("mem")
    wanted = jnp.max(
        jnp.where(peer_ids // held_blocks == mine, peer_ids % held_blocks, -1), axis=1
    )
    slot_live = jnp.where(request >= 0, jnp.clip(fills - request * BLK, 0, BLK), 0)
    key_mask = masks(slot_live, owner_shard, tokens)
    memory_here = memory_rows[0]
    width = KEY_VALUE_HEADS * DH
    wanted_hot = (wanted[:, None] == jnp.arange(held_blocks, dtype=jnp.int32)[None, :]).astype(
        jnp.bfloat16
    )
    entry_hot = (owner_shard.reshape(-1)[:, None] == shard_ids[None, :]).astype(jnp.bfloat16)
    per_chunk = 2
    chunks = KEY_VALUE_HEADS // per_chunk
    span = per_chunk * DH
    query_parts, key_parts, value_parts, owned_parts, sent_grads = [], [], [], [], []
    for chunk in range(chunks):
        first = chunk * per_chunk
        lo = first * DH
        memory_chunk = jnp.concatenate(
            [memory_here[:, :, lo : lo + span], memory_here[:, :, width + lo : width + lo + span]],
            axis=-1,
        )
        payload = jnp.take(memory_chunk, jnp.maximum(wanted, 0), axis=0)
        if chunk >= 2:
            payload, sent_grads[chunk - 2] = lax.optimization_barrier(
                (payload, sent_grads[chunk - 2])
            )
        slots = lax.all_to_all(payload, "mem", split_axis=0, concat_axis=0, tiled=True)
        chosen = jnp.einsum(
            "es,stx->etx", entry_hot, slots, preferred_element_type=jnp.bfloat16
        ).reshape(qblocks, memory_len, 2, per_chunk, DH)
        mem_keys = jnp.transpose(chosen[:, :, 0], (2, 0, 1, 3))
        mem_values = jnp.transpose(chosen[:, :, 1], (2, 0, 1, 3))
        local_keys = jnp.transpose(keys_local[:, first : first + per_chunk], (1, 0, 2))
        local_values = jnp.transpose(values_local[:, first : first + per_chunk], (1, 0, 2))
        key_rows = jnp.concatenate(
            [mem_keys, jnp.broadcast_to(local_keys[:, None], (per_chunk, qblocks, tokens, DH))],
            axis=2,
        )
        value_rows = jnp.concatenate(
            [mem_values, jnp.broadcast_to(local_values[:, None], (per_chunk, qblocks, tokens, DH))],
            axis=2,
        )
        queries_chunk = queries[:, :, first : first + per_chunk]
        grads_chunk = grad_rows[:, :, first : first + per_chunk]
        log_total, attended = head_forward(key_mask, (queries_chunk, key_rows, value_rows))
        grad_query, grad_key, grad_value = head_backward(
            key_mask,
            (queries_chunk, key_rows, value_rows, grads_chunk, log_total, attended),
        )
        query_parts.append(grad_query.reshape(tokens, per_chunk * groups * DH))
        key_parts.append(
            jnp.transpose(jnp.sum(grad_key[:, :, memory_len:], axis=1), (1, 0, 2)).reshape(
                tokens, span
            )
        )
        value_parts.append(
            jnp.transpose(jnp.sum(grad_value[:, :, memory_len:], axis=1), (1, 0, 2)).reshape(
                tokens, span
            )
        )
        entry_grads = jnp.stack(
            [grad_key[:, :, :memory_len], grad_value[:, :, :memory_len]], axis=0
        )
        entry_grads = jnp.transpose(
            entry_grads.reshape(2, per_chunk, qblocks * topk, BLK, DH), (2, 3, 0, 1, 4)
        ).reshape(qblocks * topk, BLK, 2 * span)
        slot_grads = jnp.einsum(
            "es,etx->stx",
            entry_hot.astype(jnp.float32),
            entry_grads,
            precision=lax.Precision.HIGHEST,
            preferred_element_type=jnp.float32,
        ).astype(jnp.bfloat16)
        sent_grads.append(slot_grads)
    for chunk in range(chunks):
        received = lax.all_to_all(
            sent_grads[chunk], "mem", split_axis=0, concat_axis=0, tiled=True
        )
        owned = jnp.einsum(
            "rj,rtx->jtx", wanted_hot, received, preferred_element_type=jnp.float32
        )
        owned_parts.append(lax.psum(owned.astype(jnp.bfloat16), "dp"))
    section_grads = jnp.concatenate(query_parts + key_parts + value_parts, axis=-1).astype(
        jnp.bfloat16
    )
    upstream = passed_along(section_grads[None, None], "section", -1)
    summed = jnp.concatenate(
        [part[:, :, :span] for part in owned_parts] + [part[:, :, span:] for part in owned_parts],
        axis=-1,
    )
    memory_grad = summed[None]
    return (upstream, memory_grad)


def solution(mesh):
    placed = (
        P("section", ("dp", "mem"), None, None),
        P("section", ("dp", "mem"), None, None),
        P("section", "mem", None, None),
        P("section", "mem"),
        P("section", ("dp", "mem"), None, None),
    )
    return jax.shard_map(
        per_device,
        mesh=mesh,
        in_specs=placed,
        out_specs=(P("section", ("dp", "mem"), None, None), P("section", "mem", None, None)),
        check_vma=False,
    )
```

```python
from functools import partial

import jax
import jax.numpy as jnp
from jax import lax
from jax.sharding import PartitionSpec as P

H = 16
KEY_VALUE_HEADS = 4
DH = 128
BLK = 64


NEG_FILL = -1e30


def passed_along(array, axis, by):
    devices = lax.axis_size(axis)
    pairs = [(i, i + by) for i in range(devices) if 0 <= i + by < devices]
    return lax.ppermute(array, axis, pairs)


def head_scores(key_mask, queries, key_rows):
    raw = jnp.einsum(
        "bighd,gbnd->bighn", queries, key_rows, preferred_element_type=jnp.float32
    ) * DH ** (-0.5)
    return jnp.where(key_mask[:, :, None, None, :], raw, NEG_FILL)


def head_forward(key_mask, pieces):
    queries, key_rows, value_rows = pieces
    scores = head_scores(key_mask, queries, key_rows)
    row_max = jnp.max(scores, axis=-1, keepdims=True)
    log_total = row_max + jnp.log(jnp.sum(jnp.exp(scores - row_max), axis=-1, keepdims=True))
    prob_bf = jnp.exp(scores - log_total).astype(jnp.bfloat16)
    attended = jnp.einsum(
        "bighn,gbnd->bighd", prob_bf, value_rows, preferred_element_type=jnp.float32
    ).astype(jnp.bfloat16)
    return (log_total, attended)


def head_backward(key_mask, pieces):
    queries, key_rows, value_rows, grad_rows, log_total, attended = pieces
    scores = head_scores(key_mask, queries, key_rows)
    weights = jnp.exp(scores - log_total)
    prob_bf = weights.astype(jnp.bfloat16)
    dprobs = jnp.einsum("bighd,gbnd->bighn", grad_rows, value_rows, preferred_element_type=jnp.float32)
    row_delta = jnp.sum(
        grad_rows.astype(jnp.float32) * attended.astype(jnp.float32), axis=-1, keepdims=True
    )
    dscores = (weights * (dprobs - row_delta)).astype(jnp.bfloat16)
    inv_root = DH ** (-0.5)
    grad_query = (
        jnp.einsum("bighn,gbnd->bighd", dscores, key_rows, preferred_element_type=jnp.float32)
        * inv_root
    )
    grad_key = (
        jnp.einsum("bighn,bighd->gbnd", dscores, queries, preferred_element_type=jnp.float32)
        * inv_root
    )
    grad_value = jnp.einsum(
        "bighn,bighd->gbnd", prob_bf, grad_rows, preferred_element_type=jnp.float32
    )
    return (grad_query, grad_key, grad_value)


def masks(slot_live, owner_shard, tokens):
    qblocks, topk = owner_shard.shape
    memory_len = topk * BLK
    live_len = jnp.take(slot_live, owner_shard.reshape(-1))
    live_mask = (jnp.arange(BLK)[None, :] < live_len[:, None]).reshape(qblocks, memory_len)
    row_pos = jnp.arange(qblocks)[:, None] * BLK + jnp.arange(BLK)[None, :]
    causal = jnp.arange(tokens)[None, None, :] <= row_pos[:, :, None]
    return jnp.concatenate(
        [jnp.broadcast_to(live_mask[:, None, :], (qblocks, BLK, memory_len)), causal], axis=-1
    )


def per_device(qkv_rows, grad_output, memory_rows, shard_fill, block_ids):
    shards = lax.axis_size("mem")
    groups = H // KEY_VALUE_HEADS
    rows_here = qkv_rows[0, 0]
    tokens = rows_here.shape[0]
    ids_here = block_ids[0, 0]
    qblocks, topk = ids_here.shape
    memory_len = topk * BLK
    held_blocks = memory_rows.shape[1]
    queries = rows_here[:, : H * DH].reshape(qblocks, BLK, KEY_VALUE_HEADS, groups, DH)
    keys_local = rows_here[:, H * DH : (H + KEY_VALUE_HEADS) * DH].reshape(
        tokens, KEY_VALUE_HEADS, DH
    )
    values_local = rows_here[:, (H + KEY_VALUE_HEADS) * DH :].reshape(tokens, KEY_VALUE_HEADS, DH)
    grad_rows = grad_output[0, 0].reshape(qblocks, BLK, KEY_VALUE_HEADS, groups, DH)
    owner_shard = ids_here // held_blocks
    slot_index = ids_here % held_blocks
    shard_ids = jnp.arange(shards, dtype=jnp.int32)
    hits = owner_shard[:, :, None] == shard_ids[None, None, :]
    request = jnp.max(jnp.where(hits, slot_index[:, :, None], -1), axis=(0, 1))
    asks = jnp.stack([request, jnp.broadcast_to(shard_fill[0, 0], (shards,))], axis=1)
    answers = lax.all_to_all(asks, "mem", split_axis=0, concat_axis=0, tiled=True)
    wanted = answers[:, 0]
    fills = answers[:, 1]
    slot_live = jnp.where(request >= 0, jnp.clip(fills - request * BLK, 0, BLK), 0)
    key_mask = masks(slot_live, owner_shard, tokens)
    memory_here = memory_rows[0]
    width = KEY_VALUE_HEADS * DH
    wanted_hot = (wanted[:, None] == jnp.arange(held_blocks, dtype=jnp.int32)[None, :]).astype(
        jnp.bfloat16
    )
    entry_hot = (owner_shard.reshape(-1)[:, None] == shard_ids[None, :]).astype(jnp.bfloat16)
    per_chunk = 2
    chunks = KEY_VALUE_HEADS // per_chunk
    span = per_chunk * DH
    query_parts, key_parts, value_parts, owned_parts, sent_grads = [], [], [], [], []
    for chunk in range(chunks):
        first = chunk * per_chunk
        lo = first * DH
        memory_chunk = jnp.concatenate(
            [memory_here[:, :, lo : lo + span], memory_here[:, :, width + lo : width + lo + span]],
            axis=-1,
        )
        payload = jnp.einsum(
            "rj,jtx->rtx", wanted_hot, memory_chunk, preferred_element_type=jnp.bfloat16
        )
        if chunk >= 2:
            payload, sent_grads[chunk - 2] = lax.optimization_barrier(
                (payload, sent_grads[chunk - 2])
            )
        slots = lax.all_to_all(payload, "mem", split_axis=0, concat_axis=0, tiled=True)
        chosen = jnp.einsum(
            "es,stx->etx", entry_hot, slots, preferred_element_type=jnp.bfloat16
        ).reshape(qblocks, memory_len, 2, per_chunk, DH)
        mem_keys = jnp.transpose(chosen[:, :, 0], (2, 0, 1, 3))
        mem_values = jnp.transpose(chosen[:, :, 1], (2, 0, 1, 3))
        local_keys = jnp.transpose(keys_local[:, first : first + per_chunk], (1, 0, 2))
        local_values = jnp.transpose(values_local[:, first : first + per_chunk], (1, 0, 2))
        key_rows = jnp.concatenate(
            [mem_keys, jnp.broadcast_to(local_keys[:, None], (per_chunk, qblocks, tokens, DH))],
            axis=2,
        )
        value_rows = jnp.concatenate(
            [mem_values, jnp.broadcast_to(local_values[:, None], (per_chunk, qblocks, tokens, DH))],
            axis=2,
        )
        queries_chunk = queries[:, :, first : first + per_chunk]
        grads_chunk = grad_rows[:, :, first : first + per_chunk]
        log_total, attended = head_forward(key_mask, (queries_chunk, key_rows, value_rows))
        grad_query, grad_key, grad_value = head_backward(
            key_mask,
            (queries_chunk, key_rows, value_rows, grads_chunk, log_total, attended),
        )
        query_parts.append(grad_query.reshape(tokens, per_chunk * groups * DH))
        key_parts.append(
            jnp.transpose(jnp.sum(grad_key[:, :, memory_len:], axis=1), (1, 0, 2)).reshape(
                tokens, span
            )
        )
        value_parts.append(
            jnp.transpose(jnp.sum(grad_value[:, :, memory_len:], axis=1), (1, 0, 2)).reshape(
                tokens, span
            )
        )
        entry_grads = jnp.stack(
            [grad_key[:, :, :memory_len], grad_value[:, :, :memory_len]], axis=0
        )
        entry_grads = jnp.transpose(
            entry_grads.reshape(2, per_chunk, qblocks * topk, BLK, DH), (2, 3, 0, 1, 4)
        ).reshape(qblocks * topk, BLK, 2 * span)
        slot_grads = jnp.einsum(
            "es,etx->stx",
            entry_hot.astype(jnp.float32),
            entry_grads,
            precision=lax.Precision.HIGHEST,
            preferred_element_type=jnp.float32,
        ).astype(jnp.bfloat16)
        sent_grads.append(slot_grads)
    for chunk in range(chunks):
        received = lax.all_to_all(
            sent_grads[chunk], "mem", split_axis=0, concat_axis=0, tiled=True
        )
        owned = jnp.einsum(
            "rj,rtx->jtx", wanted_hot, received, preferred_element_type=jnp.float32
        )
        partner = lax.ppermute(owned, "dp", [(0, 1), (1, 0)])
        owned_parts.append(owned + partner)
    section_grads = jnp.concatenate(query_parts + key_parts + value_parts, axis=-1).astype(
        jnp.bfloat16
    )
    upstream = passed_along(section_grads[None, None], "section", -1)
    summed = jnp.concatenate(
        [part[:, :, :span] for part in owned_parts] + [part[:, :, span:] for part in owned_parts],
        axis=-1,
    )
    memory_grad = summed.astype(jnp.bfloat16)[None]
    return (upstream, memory_grad)


def solution(mesh):
    placed = (
        P("section", ("dp", "mem"), None, None),
        P("section", ("dp", "mem"), None, None),
        P("section", "mem", None, None),
        P("section", "mem"),
        P("section", ("dp", "mem"), None, None),
    )
    return jax.shard_map(
        per_device,
        mesh=mesh,
        in_specs=placed,
        out_specs=(P("section", ("dp", "mem"), None, None), P("section", "mem", None, None)),
        check_vma=False,
    )
```

```python
from functools import partial

import jax
import jax.numpy as jnp
from jax import lax
from jax.sharding import PartitionSpec as P

H = 16
KEY_VALUE_HEADS = 4
DH = 128
BLK = 64


NEG_FILL = -1e30


def passed_along(array, axis, by):
    devices = lax.axis_size(axis)
    pairs = [(i, i + by) for i in range(devices) if 0 <= i + by < devices]
    return lax.ppermute(array, axis, pairs)


def head_scores(key_mask, queries, key_rows):
    raw = jnp.einsum(
        "bighd,gbnd->bighn", queries, key_rows, preferred_element_type=jnp.float32
    ) * DH ** (-0.5)
    return jnp.where(key_mask[:, :, None, None, :], raw, NEG_FILL)


def head_forward(key_mask, pieces):
    queries, key_rows, value_rows = pieces
    scores = head_scores(key_mask, queries, key_rows)
    row_max = jnp.max(scores, axis=-1, keepdims=True)
    log_total = row_max + jnp.log(jnp.sum(jnp.exp(scores - row_max), axis=-1, keepdims=True))
    prob_bf = jnp.exp(scores - log_total).astype(jnp.bfloat16)
    attended = jnp.einsum(
        "bighn,gbnd->bighd", prob_bf, value_rows, preferred_element_type=jnp.float32
    ).astype(jnp.bfloat16)
    return (log_total, attended)


def head_backward(key_mask, pieces):
    queries, key_rows, value_rows, grad_rows, log_total, attended = pieces
    scores = head_scores(key_mask, queries, key_rows)
    weights = jnp.exp(scores - log_total)
    prob_bf = weights.astype(jnp.bfloat16)
    dprobs = jnp.einsum("bighd,gbnd->bighn", grad_rows, value_rows, preferred_element_type=jnp.float32)
    row_delta = jnp.sum(
        grad_rows.astype(jnp.float32) * attended.astype(jnp.float32), axis=-1, keepdims=True
    )
    dscores = (weights * (dprobs - row_delta)).astype(jnp.bfloat16)
    inv_root = DH ** (-0.5)
    grad_query = (
        jnp.einsum("bighn,gbnd->bighd", dscores, key_rows, preferred_element_type=jnp.float32)
        * inv_root
    )
    grad_key = (
        jnp.einsum("bighn,bighd->gbnd", dscores, queries, preferred_element_type=jnp.float32)
        * inv_root
    )
    grad_value = jnp.einsum(
        "bighn,bighd->gbnd", prob_bf, grad_rows, preferred_element_type=jnp.float32
    )
    return (grad_query, grad_key, grad_value)


def masks(slot_live, owner_shard, tokens):
    qblocks, topk = owner_shard.shape
    memory_len = topk * BLK
    live_len = jnp.take(slot_live, owner_shard.reshape(-1))
    live_mask = (jnp.arange(BLK)[None, :] < live_len[:, None]).reshape(qblocks, memory_len)
    row_pos = jnp.arange(qblocks)[:, None] * BLK + jnp.arange(BLK)[None, :]
    causal = jnp.arange(tokens)[None, None, :] <= row_pos[:, :, None]
    return jnp.concatenate(
        [jnp.broadcast_to(live_mask[:, None, :], (qblocks, BLK, memory_len)), causal], axis=-1
    )


def per_device(qkv_rows, grad_output, memory_rows, shard_fill, block_ids):
    shards = lax.axis_size("mem")
    groups = H // KEY_VALUE_HEADS
    rows_here = qkv_rows[0, 0]
    tokens = rows_here.shape[0]
    ids_here = block_ids[0, 0]
    qblocks, topk = ids_here.shape
    memory_len = topk * BLK
    held_blocks = memory_rows.shape[1]
    queries = rows_here[:, : H * DH].reshape(qblocks, BLK, KEY_VALUE_HEADS, groups, DH)
    keys_local = rows_here[:, H * DH : (H + KEY_VALUE_HEADS) * DH].reshape(
        tokens, KEY_VALUE_HEADS, DH
    )
    values_local = rows_here[:, (H + KEY_VALUE_HEADS) * DH :].reshape(tokens, KEY_VALUE_HEADS, DH)
    grad_rows = grad_output[0, 0].reshape(qblocks, BLK, KEY_VALUE_HEADS, groups, DH)
    owner_shard = ids_here // held_blocks
    slot_index = ids_here % held_blocks
    shard_ids = jnp.arange(shards, dtype=jnp.int32)
    hits = owner_shard[:, :, None] == shard_ids[None, None, :]
    request = jnp.max(jnp.where(hits, slot_index[:, :, None], -1), axis=(0, 1))
    asks = jnp.stack([request, jnp.broadcast_to(shard_fill[0, 0], (shards,))], axis=1)
    answers = lax.all_to_all(asks, "mem", split_axis=0, concat_axis=0, tiled=True)
    wanted = answers[:, 0]
    fills = answers[:, 1]
    slot_live = jnp.where(request >= 0, jnp.clip(fills - request * BLK, 0, BLK), 0)
    key_mask = masks(slot_live, owner_shard, tokens)
    memory_here = memory_rows[0]
    width = KEY_VALUE_HEADS * DH
    wanted_hot = (wanted[:, None] == jnp.arange(held_blocks, dtype=jnp.int32)[None, :]).astype(
        jnp.bfloat16
    )
    entry_hot = (owner_shard.reshape(-1)[:, None] == shard_ids[None, :]).astype(jnp.bfloat16)
    per_chunk = 2
    chunks = KEY_VALUE_HEADS // per_chunk
    span = per_chunk * DH
    query_parts, key_parts, value_parts, owned_parts, sent_grads = [], [], [], [], []
    for chunk in range(chunks):
        first = chunk * per_chunk
        lo = first * DH
        memory_chunk = jnp.concatenate(
            [memory_here[:, :, lo : lo + span], memory_here[:, :, width + lo : width + lo + span]],
            axis=-1,
        )
        payload = memory_chunk.at[jnp.maximum(wanted, 0)].get(mode="promise_in_bounds")
        if chunk >= 2:
            payload, sent_grads[chunk - 2] = lax.optimization_barrier(
                (payload, sent_grads[chunk - 2])
            )
        slots = lax.all_to_all(payload, "mem", split_axis=0, concat_axis=0, tiled=True)
        chosen = jnp.einsum(
            "es,stx->etx", entry_hot, slots, preferred_element_type=jnp.bfloat16
        ).reshape(qblocks, memory_len, 2, per_chunk, DH)
        mem_keys = jnp.transpose(chosen[:, :, 0], (2, 0, 1, 3))
        mem_values = jnp.transpose(chosen[:, :, 1], (2, 0, 1, 3))
        local_keys = jnp.transpose(keys_local[:, first : first + per_chunk], (1, 0, 2))
        local_values = jnp.transpose(values_local[:, first : first + per_chunk], (1, 0, 2))
        key_rows = jnp.concatenate(
            [mem_keys, jnp.broadcast_to(local_keys[:, None], (per_chunk, qblocks, tokens, DH))],
            axis=2,
        )
        value_rows = jnp.concatenate(
            [mem_values, jnp.broadcast_to(local_values[:, None], (per_chunk, qblocks, tokens, DH))],
            axis=2,
        )
        queries_chunk = queries[:, :, first : first + per_chunk]
        grads_chunk = grad_rows[:, :, first : first + per_chunk]
        log_total, attended = head_forward(key_mask, (queries_chunk, key_rows, value_rows))
        grad_query, grad_key, grad_value = head_backward(
            key_mask,
            (queries_chunk, key_rows, value_rows, grads_chunk, log_total, attended),
        )
        query_parts.append(grad_query.reshape(tokens, per_chunk * groups * DH))
        key_parts.append(
            jnp.transpose(jnp.sum(grad_key[:, :, memory_len:], axis=1), (1, 0, 2)).reshape(
                tokens, span
            )
        )
        value_parts.append(
            jnp.transpose(jnp.sum(grad_value[:, :, memory_len:], axis=1), (1, 0, 2)).reshape(
                tokens, span
            )
        )
        entry_grads = jnp.stack(
            [grad_key[:, :, :memory_len], grad_value[:, :, :memory_len]], axis=0
        )
        entry_grads = jnp.transpose(
            entry_grads.reshape(2, per_chunk, qblocks * topk, BLK, DH), (2, 3, 0, 1, 4)
        ).reshape(qblocks * topk, BLK, 2 * span)
        slot_grads = jnp.einsum(
            "es,etx->stx",
            entry_hot.astype(jnp.float32),
            entry_grads,
            precision=lax.Precision.HIGHEST,
            preferred_element_type=jnp.float32,
        ).astype(jnp.bfloat16)
        sent_grads.append(slot_grads)
    for chunk in range(chunks):
        received = lax.all_to_all(
            sent_grads[chunk], "mem", split_axis=0, concat_axis=0, tiled=True
        )
        owned = jnp.einsum(
            "rj,rtx->jtx", wanted_hot, received, preferred_element_type=jnp.float32
        )
        partner = lax.ppermute(owned, "dp", [(0, 1), (1, 0)])
        owned_parts.append(owned + partner)
    section_grads = jnp.concatenate(query_parts + key_parts + value_parts, axis=-1).astype(
        jnp.bfloat16
    )
    upstream = passed_along(section_grads[None, None], "section", -1)
    summed = jnp.concatenate(
        [part[:, :, :span] for part in owned_parts] + [part[:, :, span:] for part in owned_parts],
        axis=-1,
    )
    memory_grad = summed.astype(jnp.bfloat16)[None]
    return (upstream, memory_grad)


def solution(mesh):
    placed = (
        P("section", ("dp", "mem"), None, None),
        P("section", ("dp", "mem"), None, None),
        P("section", "mem", None, None),
        P("section", "mem"),
        P("section", ("dp", "mem"), None, None),
    )
    return jax.shard_map(
        per_device,
        mesh=mesh,
        in_specs=placed,
        out_specs=(P("section", ("dp", "mem"), None, None), P("section", "mem", None, None)),
        check_vma=False,
    )
```

```python
from functools import partial

import jax
import jax.numpy as jnp
from jax import lax
from jax.sharding import PartitionSpec as P

H = 16
KEY_VALUE_HEADS = 4
DH = 128
BLK = 64


NEG_FILL = -1e30


def passed_along(array, axis, by):
    devices = lax.axis_size(axis)
    pairs = [(i, i + by) for i in range(devices) if 0 <= i + by < devices]
    return lax.ppermute(array, axis, pairs)


def head_scores(key_mask, queries, key_rows):
    raw = jnp.einsum(
        "bighd,gbnd->bighn", queries, key_rows, preferred_element_type=jnp.float32
    ) * DH ** (-0.5)
    return jnp.where(key_mask[:, :, None, None, :], raw, NEG_FILL)


def head_forward(key_mask, pieces):
    queries, key_rows, value_rows = pieces
    scores = head_scores(key_mask, queries, key_rows)
    row_max = jnp.max(scores, axis=-1, keepdims=True)
    log_total = row_max + jnp.log(jnp.sum(jnp.exp(scores - row_max), axis=-1, keepdims=True))
    prob_bf = jnp.exp(scores - log_total).astype(jnp.bfloat16)
    attended = jnp.einsum(
        "bighn,gbnd->bighd", prob_bf, value_rows, preferred_element_type=jnp.float32
    ).astype(jnp.bfloat16)
    return (log_total, attended)


def head_backward(key_mask, pieces):
    queries, key_rows, value_rows, grad_rows, log_total, attended = pieces
    scores = head_scores(key_mask, queries, key_rows)
    weights = jnp.exp(scores - log_total)
    prob_bf = weights.astype(jnp.bfloat16)
    dprobs = jnp.einsum("bighd,gbnd->bighn", grad_rows, value_rows, preferred_element_type=jnp.float32)
    row_delta = jnp.sum(
        grad_rows.astype(jnp.float32) * attended.astype(jnp.float32), axis=-1, keepdims=True
    )
    dscores = (weights * (dprobs - row_delta)).astype(jnp.bfloat16)
    inv_root = DH ** (-0.5)
    grad_query = (
        jnp.einsum("bighn,gbnd->bighd", dscores, key_rows, preferred_element_type=jnp.float32)
        * inv_root
    )
    grad_key = (
        jnp.einsum("bighn,bighd->gbnd", dscores, queries, preferred_element_type=jnp.float32)
        * inv_root
    )
    grad_value = jnp.einsum(
        "bighn,bighd->gbnd", prob_bf, grad_rows, preferred_element_type=jnp.float32
    )
    return (grad_query, grad_key, grad_value)


def masks(slot_live, owner_shard, tokens):
    qblocks, topk = owner_shard.shape
    memory_len = topk * BLK
    live_len = jnp.take(slot_live, owner_shard.reshape(-1))
    live_mask = (jnp.arange(BLK)[None, :] < live_len[:, None]).reshape(qblocks, memory_len)
    row_pos = jnp.arange(qblocks)[:, None] * BLK + jnp.arange(BLK)[None, :]
    causal = jnp.arange(tokens)[None, None, :] <= row_pos[:, :, None]
    return jnp.concatenate(
        [jnp.broadcast_to(live_mask[:, None, :], (qblocks, BLK, memory_len)), causal], axis=-1
    )


def per_device(qkv_rows, grad_output, memory_rows, shard_fill, block_ids):
    shards = lax.axis_size("mem")
    groups = H // KEY_VALUE_HEADS
    rows_here = qkv_rows[0, 0]
    tokens = rows_here.shape[0]
    ids_here = block_ids[0, 0]
    qblocks, topk = ids_here.shape
    memory_len = topk * BLK
    held_blocks = memory_rows.shape[1]
    queries = rows_here[:, : H * DH].reshape(qblocks, BLK, KEY_VALUE_HEADS, groups, DH)
    keys_local = rows_here[:, H * DH : (H + KEY_VALUE_HEADS) * DH].reshape(
        tokens, KEY_VALUE_HEADS, DH
    )
    values_local = rows_here[:, (H + KEY_VALUE_HEADS) * DH :].reshape(tokens, KEY_VALUE_HEADS, DH)
    grad_rows = grad_output[0, 0].reshape(qblocks, BLK, KEY_VALUE_HEADS, groups, DH)
    owner_shard = ids_here // held_blocks
    slot_index = ids_here % held_blocks
    shard_ids = jnp.arange(shards, dtype=jnp.int32)
    hits = owner_shard[:, :, None] == shard_ids[None, None, :]
    request = jnp.max(jnp.where(hits, slot_index[:, :, None], -1), axis=(0, 1))
    asks = jnp.stack([request, jnp.broadcast_to(shard_fill[0, 0], (shards,))], axis=1)
    answers = lax.all_to_all(asks, "mem", split_axis=0, concat_axis=0, tiled=True)
    wanted = answers[:, 0]
    fills = answers[:, 1]
    slot_live = jnp.where(request >= 0, jnp.clip(fills - request * BLK, 0, BLK), 0)
    key_mask = masks(slot_live, owner_shard, tokens)
    memory_here = memory_rows[0]
    width = KEY_VALUE_HEADS * DH
    wanted_hot = (wanted[:, None] == jnp.arange(held_blocks, dtype=jnp.int32)[None, :]).astype(
        jnp.bfloat16
    )
    owner_flat = owner_shard.reshape(-1)
    key_slot = jnp.sum(jnp.where(hits, jnp.arange(topk, dtype=jnp.int32)[None, :, None], 0), axis=1)
    present = jnp.any(hits, axis=1)
    per_chunk = 2
    chunks = KEY_VALUE_HEADS // per_chunk
    span = per_chunk * DH
    query_parts, key_parts, value_parts, owned_parts, sent_grads = [], [], [], [], []
    for chunk in range(chunks):
        first = chunk * per_chunk
        lo = first * DH
        memory_chunk = jnp.concatenate(
            [memory_here[:, :, lo : lo + span], memory_here[:, :, width + lo : width + lo + span]],
            axis=-1,
        )
        payload = memory_chunk.at[jnp.maximum(wanted, 0)].get(mode="promise_in_bounds")
        if chunk >= 2:
            payload, sent_grads[chunk - 2] = lax.optimization_barrier(
                (payload, sent_grads[chunk - 2])
            )
        slots = lax.all_to_all(payload, "mem", split_axis=0, concat_axis=0, tiled=True)
        if chunk >= 1:
            slots, sent_grads[chunk - 1] = lax.optimization_barrier(
                (slots, sent_grads[chunk - 1])
            )
        chosen = slots.at[owner_flat].get(mode="promise_in_bounds").reshape(
            qblocks, memory_len, 2, per_chunk, DH
        )
        mem_keys = jnp.transpose(chosen[:, :, 0], (2, 0, 1, 3))
        mem_values = jnp.transpose(chosen[:, :, 1], (2, 0, 1, 3))
        local_keys = jnp.transpose(keys_local[:, first : first + per_chunk], (1, 0, 2))
        local_values = jnp.transpose(values_local[:, first : first + per_chunk], (1, 0, 2))
        key_rows = jnp.concatenate(
            [mem_keys, jnp.broadcast_to(local_keys[:, None], (per_chunk, qblocks, tokens, DH))],
            axis=2,
        )
        value_rows = jnp.concatenate(
            [mem_values, jnp.broadcast_to(local_values[:, None], (per_chunk, qblocks, tokens, DH))],
            axis=2,
        )
        queries_chunk = queries[:, :, first : first + per_chunk]
        grads_chunk = grad_rows[:, :, first : first + per_chunk]
        log_total, attended = head_forward(key_mask, (queries_chunk, key_rows, value_rows))
        grad_query, grad_key, grad_value = head_backward(
            key_mask,
            (queries_chunk, key_rows, value_rows, grads_chunk, log_total, attended),
        )
        query_parts.append(grad_query.reshape(tokens, per_chunk * groups * DH))
        key_parts.append(
            jnp.transpose(jnp.sum(grad_key[:, :, memory_len:], axis=1), (1, 0, 2)).reshape(
                tokens, span
            )
        )
        value_parts.append(
            jnp.transpose(jnp.sum(grad_value[:, :, memory_len:], axis=1), (1, 0, 2)).reshape(
                tokens, span
            )
        )
        entry_grads = jnp.stack(
            [grad_key[:, :, :memory_len], grad_value[:, :, :memory_len]], axis=0
        )
        entry_grads = jnp.transpose(
            entry_grads.reshape(2, per_chunk, qblocks * topk, BLK, DH), (2, 3, 0, 1, 4)
        ).reshape(qblocks * topk, BLK, 2 * span)
        by_block = entry_grads.reshape(qblocks, topk, BLK, 2 * span)
        slot_grads = sum(
            jnp.where(
                present[block][:, None, None],
                by_block[block].at[key_slot[block]].get(mode="promise_in_bounds"),
                jnp.float32(0.0),
            )
            for block in range(qblocks)
        ).astype(jnp.bfloat16)
        sent_grads.append(slot_grads)
    for chunk in range(chunks):
        received = lax.all_to_all(
            sent_grads[chunk], "mem", split_axis=0, concat_axis=0, tiled=True
        )
        owned = jnp.einsum(
            "rj,rtx->jtx", wanted_hot, received, preferred_element_type=jnp.float32
        )
        partner = lax.ppermute(owned, "dp", [(0, 1), (1, 0)])
        owned_parts.append(owned + partner)
    section_grads = jnp.concatenate(query_parts + key_parts + value_parts, axis=-1).astype(
        jnp.bfloat16
    )
    upstream = passed_along(section_grads[None, None], "section", -1)
    summed = jnp.concatenate(
        [part[:, :, :span] for part in owned_parts] + [part[:, :, span:] for part in owned_parts],
        axis=-1,
    )
    memory_grad = summed.astype(jnp.bfloat16)[None]
    return (upstream, memory_grad)


def solution(mesh):
    placed = (
        P("section", ("dp", "mem"), None, None),
        P("section", ("dp", "mem"), None, None),
        P("section", "mem", None, None),
        P("section", "mem"),
        P("section", ("dp", "mem"), None, None),
    )
    return jax.shard_map(
        per_device,
        mesh=mesh,
        in_specs=placed,
        out_specs=(P("section", ("dp", "mem"), None, None), P("section", "mem", None, None)),
        check_vma=False,
    )
```

```python
from functools import partial

import jax
import jax.numpy as jnp
from jax import lax
from jax.sharding import PartitionSpec as P

H = 16
KEY_VALUE_HEADS = 4
DH = 128
BLK = 64


NEG_FILL = -1e30


def passed_along(array, axis, by):
    devices = lax.axis_size(axis)
    pairs = [(i, i + by) for i in range(devices) if 0 <= i + by < devices]
    return lax.ppermute(array, axis, pairs)


def head_scores(key_mask, queries, key_rows):
    raw = jnp.einsum(
        "bighd,gbnd->bighn", queries, key_rows, preferred_element_type=jnp.float32
    ) * DH ** (-0.5)
    return jnp.where(key_mask[:, :, None, None, :], raw, NEG_FILL)


def head_forward(key_mask, pieces):
    queries, key_rows, value_rows = pieces
    scores = head_scores(key_mask, queries, key_rows)
    row_max = jnp.max(scores, axis=-1, keepdims=True)
    log_total = row_max + jnp.log(jnp.sum(jnp.exp(scores - row_max), axis=-1, keepdims=True))
    prob_bf = jnp.exp(scores - log_total).astype(jnp.bfloat16)
    attended = jnp.einsum(
        "bighn,gbnd->bighd", prob_bf, value_rows, preferred_element_type=jnp.float32
    ).astype(jnp.bfloat16)
    return (log_total, attended)


def head_backward(key_mask, pieces):
    queries, key_rows, value_rows, grad_rows, log_total, attended = pieces
    scores = head_scores(key_mask, queries, key_rows)
    weights = jnp.exp(scores - log_total)
    prob_bf = weights.astype(jnp.bfloat16)
    dprobs = jnp.einsum("bighd,gbnd->bighn", grad_rows, value_rows, preferred_element_type=jnp.float32)
    row_delta = jnp.sum(
        grad_rows.astype(jnp.float32) * attended.astype(jnp.float32), axis=-1, keepdims=True
    )
    dscores = (weights * (dprobs - row_delta)).astype(jnp.bfloat16)
    inv_root = DH ** (-0.5)
    grad_query = (
        jnp.einsum("bighn,gbnd->bighd", dscores, key_rows, preferred_element_type=jnp.float32)
        * inv_root
    )
    grad_key = (
        jnp.einsum("bighn,bighd->bngd", dscores, queries, preferred_element_type=jnp.float32)
        * inv_root
    )
    grad_value = jnp.einsum(
        "bighn,bighd->bngd", prob_bf, grad_rows, preferred_element_type=jnp.float32
    )
    return (grad_query, grad_key, grad_value)


def masks(slot_live, owner_shard, tokens):
    qblocks, topk = owner_shard.shape
    memory_len = topk * BLK
    live_len = jnp.take(slot_live, owner_shard.reshape(-1))
    live_mask = (jnp.arange(BLK)[None, :] < live_len[:, None]).reshape(qblocks, memory_len)
    row_pos = jnp.arange(qblocks)[:, None] * BLK + jnp.arange(BLK)[None, :]
    causal = jnp.arange(tokens)[None, None, :] <= row_pos[:, :, None]
    return jnp.concatenate(
        [jnp.broadcast_to(live_mask[:, None, :], (qblocks, BLK, memory_len)), causal], axis=-1
    )


def per_device(qkv_rows, grad_output, memory_rows, shard_fill, block_ids):
    shards = lax.axis_size("mem")
    groups = H // KEY_VALUE_HEADS
    rows_here = qkv_rows[0, 0]
    tokens = rows_here.shape[0]
    ids_here = block_ids[0, 0]
    qblocks, topk = ids_here.shape
    memory_len = topk * BLK
    held_blocks = memory_rows.shape[1]
    queries = rows_here[:, : H * DH].reshape(qblocks, BLK, KEY_VALUE_HEADS, groups, DH)
    keys_local = rows_here[:, H * DH : (H + KEY_VALUE_HEADS) * DH].reshape(
        tokens, KEY_VALUE_HEADS, DH
    )
    values_local = rows_here[:, (H + KEY_VALUE_HEADS) * DH :].reshape(tokens, KEY_VALUE_HEADS, DH)
    grad_rows = grad_output[0, 0].reshape(qblocks, BLK, KEY_VALUE_HEADS, groups, DH)
    owner_shard = ids_here // held_blocks
    slot_index = ids_here % held_blocks
    shard_ids = jnp.arange(shards, dtype=jnp.int32)
    hits = owner_shard[:, :, None] == shard_ids[None, None, :]
    request = jnp.max(jnp.where(hits, slot_index[:, :, None], -1), axis=(0, 1))
    asks = jnp.stack([request, jnp.broadcast_to(shard_fill[0, 0], (shards,))], axis=1)
    answers = lax.all_to_all(asks, "mem", split_axis=0, concat_axis=0, tiled=True)
    wanted = answers[:, 0]
    fills = answers[:, 1]
    slot_live = jnp.where(request >= 0, jnp.clip(fills - request * BLK, 0, BLK), 0)
    key_mask = masks(slot_live, owner_shard, tokens)
    memory_here = memory_rows[0]
    width = KEY_VALUE_HEADS * DH
    wanted_hot = (wanted[:, None] == jnp.arange(held_blocks, dtype=jnp.int32)[None, :]).astype(
        jnp.bfloat16
    )
    owner_flat = owner_shard.reshape(-1)
    key_slot = jnp.sum(jnp.where(hits, jnp.arange(topk, dtype=jnp.int32)[None, :, None], 0), axis=1)
    present = jnp.any(hits, axis=1)
    per_chunk = 2
    chunks = KEY_VALUE_HEADS // per_chunk
    span = per_chunk * DH
    query_parts, key_parts, value_parts, owned_parts, sent_grads = [], [], [], [], []
    for chunk in range(chunks):
        first = chunk * per_chunk
        lo = first * DH
        memory_chunk = jnp.concatenate(
            [memory_here[:, :, lo : lo + span], memory_here[:, :, width + lo : width + lo + span]],
            axis=-1,
        )
        payload = memory_chunk.at[jnp.maximum(wanted, 0)].get(mode="promise_in_bounds")
        if chunk >= 2:
            payload, sent_grads[chunk - 2] = lax.optimization_barrier(
                (payload, sent_grads[chunk - 2])
            )
        slots = lax.all_to_all(payload, "mem", split_axis=0, concat_axis=0, tiled=True)
        if chunk >= 1:
            slots, sent_grads[chunk - 1] = lax.optimization_barrier(
                (slots, sent_grads[chunk - 1])
            )
        chosen = slots.at[owner_flat].get(mode="promise_in_bounds").reshape(
            qblocks, memory_len, 2, per_chunk, DH
        )
        mem_keys = jnp.transpose(chosen[:, :, 0], (2, 0, 1, 3))
        mem_values = jnp.transpose(chosen[:, :, 1], (2, 0, 1, 3))
        local_keys = jnp.transpose(keys_local[:, first : first + per_chunk], (1, 0, 2))
        local_values = jnp.transpose(values_local[:, first : first + per_chunk], (1, 0, 2))
        key_rows = jnp.concatenate(
            [mem_keys, jnp.broadcast_to(local_keys[:, None], (per_chunk, qblocks, tokens, DH))],
            axis=2,
        )
        value_rows = jnp.concatenate(
            [mem_values, jnp.broadcast_to(local_values[:, None], (per_chunk, qblocks, tokens, DH))],
            axis=2,
        )
        queries_chunk = queries[:, :, first : first + per_chunk]
        grads_chunk = grad_rows[:, :, first : first + per_chunk]
        log_total, attended = head_forward(key_mask, (queries_chunk, key_rows, value_rows))
        grad_query, grad_key, grad_value = head_backward(
            key_mask,
            (queries_chunk, key_rows, value_rows, grads_chunk, log_total, attended),
        )
        query_parts.append(grad_query.reshape(tokens, per_chunk * groups * DH))
        key_parts.append(jnp.sum(grad_key[:, memory_len:], axis=0).reshape(tokens, span))
        value_parts.append(jnp.sum(grad_value[:, memory_len:], axis=0).reshape(tokens, span))
        entry_grads = jnp.concatenate(
            [
                grad_key[:, :memory_len].reshape(qblocks * topk, BLK, span),
                grad_value[:, :memory_len].reshape(qblocks * topk, BLK, span),
            ],
            axis=-1,
        )
        by_block = entry_grads.reshape(qblocks, topk, BLK, 2 * span)
        slot_grads = sum(
            jnp.where(
                present[block][:, None, None],
                by_block[block].at[key_slot[block]].get(mode="promise_in_bounds"),
                jnp.float32(0.0),
            )
            for block in range(qblocks)
        ).astype(jnp.bfloat16)
        sent_grads.append(slot_grads)
    for chunk in range(chunks):
        received = lax.all_to_all(
            sent_grads[chunk], "mem", split_axis=0, concat_axis=0, tiled=True
        )
        owned = jnp.einsum(
            "rj,rtx->jtx", wanted_hot, received, preferred_element_type=jnp.float32
        )
        partner = lax.ppermute(owned, "dp", [(0, 1), (1, 0)])
        owned_parts.append(owned + partner)
    section_grads = jnp.concatenate(query_parts + key_parts + value_parts, axis=-1).astype(
        jnp.bfloat16
    )
    upstream = passed_along(section_grads[None, None], "section", -1)
    summed = jnp.concatenate(
        [part[:, :, :span] for part in owned_parts] + [part[:, :, span:] for part in owned_parts],
        axis=-1,
    )
    memory_grad = summed.astype(jnp.bfloat16)[None]
    return (upstream, memory_grad)


def solution(mesh):
    placed = (
        P("section", ("dp", "mem"), None, None),
        P("section", ("dp", "mem"), None, None),
        P("section", "mem", None, None),
        P("section", "mem"),
        P("section", ("dp", "mem"), None, None),
    )
    return jax.shard_map(
        per_device,
        mesh=mesh,
        in_specs=placed,
        out_specs=(P("section", ("dp", "mem"), None, None), P("section", "mem", None, None)),
        check_vma=False,
    )
```

```python
from functools import partial

import jax
import jax.numpy as jnp
from jax import lax
from jax.sharding import PartitionSpec as P

H = 16
KEY_VALUE_HEADS = 4
DH = 128
BLK = 64


NEG_FILL = -1e30


def passed_along(array, axis, by):
    devices = lax.axis_size(axis)
    pairs = [(i, i + by) for i in range(devices) if 0 <= i + by < devices]
    return lax.ppermute(array, axis, pairs)


def head_scores(key_mask, queries, key_rows):
    raw = jnp.einsum(
        "bighd,gbnd->bighn", queries, key_rows, preferred_element_type=jnp.float32
    ) * DH ** (-0.5)
    return jnp.where(key_mask[:, :, None, None, :], raw, NEG_FILL)


def head_forward(key_mask, pieces):
    queries, key_rows, value_rows = pieces
    scores = head_scores(key_mask, queries, key_rows)
    row_max = jnp.max(scores, axis=-1, keepdims=True)
    log_total = row_max + jnp.log(jnp.sum(jnp.exp(scores - row_max), axis=-1, keepdims=True))
    prob_bf = jnp.exp(scores - log_total).astype(jnp.bfloat16)
    attended = jnp.einsum(
        "bighn,gbnd->bighd", prob_bf, value_rows, preferred_element_type=jnp.float32
    ).astype(jnp.bfloat16)
    return (log_total, attended)


def head_backward(key_mask, pieces):
    queries, key_rows, value_rows, grad_rows, log_total, attended = pieces
    scores = head_scores(key_mask, queries, key_rows)
    weights = jnp.exp(scores - log_total)
    prob_bf = weights.astype(jnp.bfloat16)
    dprobs = jnp.einsum("bighd,gbnd->bighn", grad_rows, value_rows, preferred_element_type=jnp.float32)
    row_delta = jnp.sum(
        grad_rows.astype(jnp.float32) * attended.astype(jnp.float32), axis=-1, keepdims=True
    )
    dscores = (weights * (dprobs - row_delta)).astype(jnp.bfloat16)
    inv_root = DH ** (-0.5)
    grad_query = (
        jnp.einsum("bighn,gbnd->bighd", dscores, key_rows, preferred_element_type=jnp.float32)
        * inv_root
    )
    grad_key = (
        jnp.einsum("bighn,bighd->bngd", dscores, queries, preferred_element_type=jnp.float32)
        * inv_root
    )
    grad_value = jnp.einsum(
        "bighn,bighd->bngd", prob_bf, grad_rows, preferred_element_type=jnp.float32
    )
    return (grad_query, grad_key, grad_value)


def masks(slot_live, owner_shard, tokens):
    qblocks, topk = owner_shard.shape
    memory_len = topk * BLK
    live_len = jnp.take(slot_live, owner_shard.reshape(-1))
    live_mask = (jnp.arange(BLK)[None, :] < live_len[:, None]).reshape(qblocks, memory_len)
    row_pos = jnp.arange(qblocks)[:, None] * BLK + jnp.arange(BLK)[None, :]
    causal = jnp.arange(tokens)[None, None, :] <= row_pos[:, :, None]
    return jnp.concatenate(
        [jnp.broadcast_to(live_mask[:, None, :], (qblocks, BLK, memory_len)), causal], axis=-1
    )


def per_device(qkv_rows, grad_output, memory_rows, shard_fill, block_ids):
    shards = lax.axis_size("mem")
    groups = H // KEY_VALUE_HEADS
    rows_here = qkv_rows[0, 0]
    tokens = rows_here.shape[0]
    ids_here = block_ids[0, 0]
    qblocks, topk = ids_here.shape
    memory_len = topk * BLK
    held_blocks = memory_rows.shape[1]
    queries = rows_here[:, : H * DH].reshape(qblocks, BLK, KEY_VALUE_HEADS, groups, DH)
    keys_local = rows_here[:, H * DH : (H + KEY_VALUE_HEADS) * DH].reshape(
        tokens, KEY_VALUE_HEADS, DH
    )
    values_local = rows_here[:, (H + KEY_VALUE_HEADS) * DH :].reshape(tokens, KEY_VALUE_HEADS, DH)
    grad_rows = grad_output[0, 0].reshape(qblocks, BLK, KEY_VALUE_HEADS, groups, DH)
    owner_shard = ids_here // held_blocks
    slot_index = ids_here % held_blocks
    shard_ids = jnp.arange(shards, dtype=jnp.int32)
    hits = owner_shard[:, :, None] == shard_ids[None, None, :]
    request = jnp.max(jnp.where(hits, slot_index[:, :, None], -1), axis=(0, 1))
    asks = jnp.stack([request, jnp.broadcast_to(shard_fill[0, 0], (shards,))], axis=1)
    answers = lax.all_to_all(asks, "mem", split_axis=0, concat_axis=0, tiled=True)
    wanted = answers[:, 0]
    fills = answers[:, 1]
    slot_live = jnp.where(request >= 0, jnp.clip(fills - request * BLK, 0, BLK), 0)
    key_mask = masks(slot_live, owner_shard, tokens)
    memory_here = memory_rows[0]
    width = KEY_VALUE_HEADS * DH
    wanted_hot = (wanted[:, None] == jnp.arange(held_blocks, dtype=jnp.int32)[None, :]).astype(
        jnp.bfloat16
    )
    owner_flat = owner_shard.reshape(-1)
    key_slot = jnp.sum(jnp.where(hits, jnp.arange(topk, dtype=jnp.int32)[None, :, None], 0), axis=1)
    present = jnp.any(hits, axis=1)
    per_chunk = 2
    chunks = KEY_VALUE_HEADS // per_chunk
    span = per_chunk * DH
    query_parts, key_parts, value_parts, owned_parts, sent_grads = [], [], [], [], []
    for chunk in range(chunks):
        first = chunk * per_chunk
        lo = first * DH
        memory_chunk = jnp.concatenate(
            [memory_here[:, :, lo : lo + span], memory_here[:, :, width + lo : width + lo + span]],
            axis=-1,
        )
        payload = memory_chunk.at[jnp.maximum(wanted, 0)].get(mode="promise_in_bounds")
        if chunk >= 2:
            payload, sent_grads[chunk - 2] = lax.optimization_barrier(
                (payload, sent_grads[chunk - 2])
            )
        slots = lax.all_to_all(payload, "mem", split_axis=0, concat_axis=0, tiled=True)
        if chunk >= 1:
            slots, sent_grads[chunk - 1] = lax.optimization_barrier(
                (slots, sent_grads[chunk - 1])
            )
        chosen = slots.at[owner_flat].get(mode="promise_in_bounds").reshape(
            qblocks, memory_len, 2, per_chunk, DH
        )
        mem_keys = jnp.transpose(chosen[:, :, 0], (2, 0, 1, 3))
        mem_values = jnp.transpose(chosen[:, :, 1], (2, 0, 1, 3))
        local_keys = jnp.transpose(keys_local[:, first : first + per_chunk], (1, 0, 2))
        local_values = jnp.transpose(values_local[:, first : first + per_chunk], (1, 0, 2))
        key_rows = jnp.concatenate(
            [mem_keys, jnp.broadcast_to(local_keys[:, None], (per_chunk, qblocks, tokens, DH))],
            axis=2,
        )
        value_rows = jnp.concatenate(
            [mem_values, jnp.broadcast_to(local_values[:, None], (per_chunk, qblocks, tokens, DH))],
            axis=2,
        )
        queries_chunk = queries[:, :, first : first + per_chunk]
        grads_chunk = grad_rows[:, :, first : first + per_chunk]
        log_total, attended = head_forward(key_mask, (queries_chunk, key_rows, value_rows))
        grad_query, grad_key, grad_value = head_backward(
            key_mask,
            (queries_chunk, key_rows, value_rows, grads_chunk, log_total, attended),
        )
        query_parts.append(grad_query.reshape(tokens, per_chunk * groups * DH))
        key_parts.append(jnp.sum(grad_key[:, memory_len:], axis=0).reshape(tokens, span))
        value_parts.append(jnp.sum(grad_value[:, memory_len:], axis=0).reshape(tokens, span))
        entry_grads = jnp.concatenate(
            [
                grad_key[:, :memory_len].reshape(qblocks * topk, BLK, span),
                grad_value[:, :memory_len].reshape(qblocks * topk, BLK, span),
            ],
            axis=-1,
        )
        by_block = entry_grads.reshape(qblocks, topk, BLK, 2 * span)
        slot_grads = sum(
            jnp.where(
                present[block][:, None, None],
                by_block[block].at[key_slot[block]].get(mode="promise_in_bounds"),
                jnp.float32(0.0),
            )
            for block in range(qblocks)
        ).astype(jnp.bfloat16)
        sent_grads.append(slot_grads)
    for chunk in range(chunks):
        received = lax.all_to_all(
            sent_grads[chunk], "mem", split_axis=0, concat_axis=0, tiled=True
        )
        owned = jnp.einsum(
            "rj,rtx->jtx", wanted_hot, received, preferred_element_type=jnp.float32
        )
        partner = lax.ppermute(owned, "dp", [(0, 1), (1, 0)])
        owned_parts.append(owned + partner)
    section_grads = jnp.concatenate(query_parts + key_parts + value_parts, axis=-1).astype(
        jnp.bfloat16
    )
    sections = lax.axis_size("section")
    cycled = lax.ppermute(
        section_grads, "section", [(i, (i - 1) % sections) for i in range(sections)]
    )
    last = lax.axis_index("section") == sections - 1
    upstream = jnp.where(last, jnp.zeros_like(cycled), cycled)[None, None]
    summed = jnp.concatenate(
        [part[:, :, :span] for part in owned_parts] + [part[:, :, span:] for part in owned_parts],
        axis=-1,
    )
    memory_grad = summed.astype(jnp.bfloat16)[None]
    return (upstream, memory_grad)


def solution(mesh):
    placed = (
        P("section", ("dp", "mem"), None, None),
        P("section", ("dp", "mem"), None, None),
        P("section", "mem", None, None),
        P("section", "mem"),
        P("section", ("dp", "mem"), None, None),
    )
    return jax.shard_map(
        per_device,
        mesh=mesh,
        in_specs=placed,
        out_specs=(P("section", ("dp", "mem"), None, None), P("section", "mem", None, None)),
        check_vma=False,
    )
```

```python
from functools import partial

import jax
import jax.numpy as jnp
from jax import lax
from jax.sharding import PartitionSpec as P

H = 16
KEY_VALUE_HEADS = 4
DH = 128
BLK = 64


NEG_FILL = -1e30


def passed_along(array, axis, by):
    devices = lax.axis_size(axis)
    pairs = [(i, i + by) for i in range(devices) if 0 <= i + by < devices]
    return lax.ppermute(array, axis, pairs)


def head_scores(key_mask, queries, key_rows):
    raw = jnp.einsum(
        "bighd,gbnd->bighn", queries, key_rows, preferred_element_type=jnp.float32
    ) * DH ** (-0.5)
    return jnp.where(key_mask[:, :, None, None, :], raw, NEG_FILL)


def head_forward(key_mask, pieces):
    queries, key_rows, value_rows = pieces
    scores = head_scores(key_mask, queries, key_rows)
    row_max = jnp.max(scores, axis=-1, keepdims=True)
    log_total = row_max + jnp.log(jnp.sum(jnp.exp(scores - row_max), axis=-1, keepdims=True))
    prob_bf = jnp.exp(scores - log_total).astype(jnp.bfloat16)
    attended = jnp.einsum(
        "bighn,gbnd->bighd", prob_bf, value_rows, preferred_element_type=jnp.float32
    ).astype(jnp.bfloat16)
    return (log_total, attended)


def head_backward(key_mask, pieces):
    queries, key_rows, value_rows, grad_rows, log_total, attended = pieces
    scores = head_scores(key_mask, queries, key_rows)
    weights = jnp.exp(scores - log_total)
    prob_bf = weights.astype(jnp.bfloat16)
    dprobs = jnp.einsum("bighd,gbnd->bighn", grad_rows, value_rows, preferred_element_type=jnp.float32)
    row_delta = jnp.sum(
        grad_rows.astype(jnp.float32) * attended.astype(jnp.float32), axis=-1, keepdims=True
    )
    dscores = (weights * (dprobs - row_delta)).astype(jnp.bfloat16)
    inv_root = DH ** (-0.5)
    grad_query = (
        jnp.einsum("bighn,gbnd->bighd", dscores, key_rows, preferred_element_type=jnp.float32)
        * inv_root
    )
    grad_key = (
        jnp.einsum("bighn,bighd->bngd", dscores, queries, preferred_element_type=jnp.float32)
        * inv_root
    )
    grad_value = jnp.einsum(
        "bighn,bighd->bngd", prob_bf, grad_rows, preferred_element_type=jnp.float32
    )
    return (grad_query, grad_key, grad_value)


def masks(slot_live, owner_shard, tokens):
    qblocks, topk = owner_shard.shape
    memory_len = topk * BLK
    live_len = jnp.take(slot_live, owner_shard.reshape(-1))
    live_mask = (jnp.arange(BLK)[None, :] < live_len[:, None]).reshape(qblocks, memory_len)
    row_pos = jnp.arange(qblocks)[:, None] * BLK + jnp.arange(BLK)[None, :]
    causal = jnp.arange(tokens)[None, None, :] <= row_pos[:, :, None]
    return jnp.concatenate(
        [jnp.broadcast_to(live_mask[:, None, :], (qblocks, BLK, memory_len)), causal], axis=-1
    )


def per_device(qkv_rows, grad_output, memory_rows, shard_fill, block_ids):
    shards = lax.axis_size("mem")
    groups = H // KEY_VALUE_HEADS
    rows_here = qkv_rows[0, 0]
    tokens = rows_here.shape[0]
    ids_here = block_ids[0, 0]
    qblocks, topk = ids_here.shape
    memory_len = topk * BLK
    held_blocks = memory_rows.shape[1]
    queries = rows_here[:, : H * DH].reshape(qblocks, BLK, KEY_VALUE_HEADS, groups, DH)
    keys_local = rows_here[:, H * DH : (H + KEY_VALUE_HEADS) * DH].reshape(
        tokens, KEY_VALUE_HEADS, DH
    )
    values_local = rows_here[:, (H + KEY_VALUE_HEADS) * DH :].reshape(tokens, KEY_VALUE_HEADS, DH)
    grad_rows = grad_output[0, 0].reshape(qblocks, BLK, KEY_VALUE_HEADS, groups, DH)
    owner_shard = ids_here // held_blocks
    slot_index = ids_here % held_blocks
    shard_ids = jnp.arange(shards, dtype=jnp.int32)
    hits = owner_shard[:, :, None] == shard_ids[None, None, :]
    request = jnp.max(jnp.where(hits, slot_index[:, :, None], -1), axis=(0, 1))
    asks = jnp.stack([request, jnp.broadcast_to(shard_fill[0, 0], (shards,))], axis=1)
    answers = lax.all_to_all(asks, "mem", split_axis=0, concat_axis=0, tiled=True)
    wanted = answers[:, 0]
    fills = answers[:, 1]
    slot_live = jnp.where(request >= 0, jnp.clip(fills - request * BLK, 0, BLK), 0)
    key_mask = masks(slot_live, owner_shard, tokens)
    memory_here = memory_rows[0]
    width = KEY_VALUE_HEADS * DH
    wanted_hot = (wanted[:, None] == jnp.arange(held_blocks, dtype=jnp.int32)[None, :]).astype(
        jnp.bfloat16
    )
    owner_flat = owner_shard.reshape(-1)
    key_slot = jnp.sum(jnp.where(hits, jnp.arange(topk, dtype=jnp.int32)[None, :, None], 0), axis=1)
    present = jnp.any(hits, axis=1)
    per_chunk = 2
    chunks = KEY_VALUE_HEADS // per_chunk
    span = per_chunk * DH
    query_parts, key_parts, value_parts, owned_parts, sent_grads = [], [], [], [], []
    for chunk in range(chunks):
        first = chunk * per_chunk
        lo = first * DH
        memory_chunk = jnp.concatenate(
            [memory_here[:, :, lo : lo + span], memory_here[:, :, width + lo : width + lo + span]],
            axis=-1,
        )
        payload = memory_chunk.at[jnp.maximum(wanted, 0)].get(mode="promise_in_bounds")
        if chunk >= 2:
            payload, sent_grads[chunk - 2] = lax.optimization_barrier(
                (payload, sent_grads[chunk - 2])
            )
        slots = lax.all_to_all(payload, "mem", split_axis=0, concat_axis=0, tiled=True)
        if chunk >= 1:
            slots, sent_grads[chunk - 1] = lax.optimization_barrier(
                (slots, sent_grads[chunk - 1])
            )
        chosen = slots.at[owner_flat].get(mode="promise_in_bounds").reshape(
            qblocks, memory_len, 2, per_chunk, DH
        )
        mem_keys = jnp.transpose(chosen[:, :, 0], (2, 0, 1, 3))
        mem_values = jnp.transpose(chosen[:, :, 1], (2, 0, 1, 3))
        local_keys = jnp.transpose(keys_local[:, first : first + per_chunk], (1, 0, 2))
        local_values = jnp.transpose(values_local[:, first : first + per_chunk], (1, 0, 2))
        key_rows = jnp.concatenate(
            [mem_keys, jnp.broadcast_to(local_keys[:, None], (per_chunk, qblocks, tokens, DH))],
            axis=2,
        )
        value_rows = jnp.concatenate(
            [mem_values, jnp.broadcast_to(local_values[:, None], (per_chunk, qblocks, tokens, DH))],
            axis=2,
        )
        queries_chunk = queries[:, :, first : first + per_chunk]
        grads_chunk = grad_rows[:, :, first : first + per_chunk]
        log_total, attended = head_forward(key_mask, (queries_chunk, key_rows, value_rows))
        grad_query, grad_key, grad_value = head_backward(
            key_mask,
            (queries_chunk, key_rows, value_rows, grads_chunk, log_total, attended),
        )
        query_parts.append(grad_query.reshape(tokens, per_chunk * groups * DH))
        key_parts.append(jnp.sum(grad_key[:, memory_len:], axis=0).reshape(tokens, span))
        value_parts.append(jnp.sum(grad_value[:, memory_len:], axis=0).reshape(tokens, span))
        entry_grads = jnp.concatenate(
            [
                grad_key[:, :memory_len].reshape(qblocks * topk, BLK, span),
                grad_value[:, :memory_len].reshape(qblocks * topk, BLK, span),
            ],
            axis=-1,
        )
        by_block = entry_grads.reshape(qblocks, topk, BLK, 2 * span)
        slot_grads = sum(
            jnp.where(
                present[block][:, None, None],
                by_block[block].at[key_slot[block]].get(mode="promise_in_bounds"),
                jnp.float32(0.0),
            )
            for block in range(qblocks)
        ).astype(jnp.bfloat16)
        sent_grads.append(slot_grads)
    for chunk in range(chunks):
        received = lax.all_to_all(
            sent_grads[chunk], "mem", split_axis=0, concat_axis=0, tiled=True
        )
        owned = jnp.sum(
            jnp.where(
                (wanted[None, :] == jnp.arange(held_blocks)[:, None])[:, :, None, None],
                received.astype(jnp.float32)[None],
                jnp.float32(0.0),
            ),
            axis=1,
        )
        partner = lax.ppermute(owned, "dp", [(0, 1), (1, 0)])
        owned_parts.append(owned + partner)
    section_grads = jnp.concatenate(query_parts + key_parts + value_parts, axis=-1).astype(
        jnp.bfloat16
    )
    sections = lax.axis_size("section")
    cycled = lax.ppermute(
        section_grads, "section", [(i, (i - 1) % sections) for i in range(sections)]
    )
    last = lax.axis_index("section") == sections - 1
    upstream = jnp.where(last, jnp.zeros_like(cycled), cycled)[None, None]
    summed = jnp.concatenate(
        [part[:, :, :span] for part in owned_parts] + [part[:, :, span:] for part in owned_parts],
        axis=-1,
    )
    memory_grad = summed.astype(jnp.bfloat16)[None]
    return (upstream, memory_grad)


def solution(mesh):
    placed = (
        P("section", ("dp", "mem"), None, None),
        P("section", ("dp", "mem"), None, None),
        P("section", "mem", None, None),
        P("section", "mem"),
        P("section", ("dp", "mem"), None, None),
    )
    return jax.shard_map(
        per_device,
        mesh=mesh,
        in_specs=placed,
        out_specs=(P("section", ("dp", "mem"), None, None), P("section", "mem", None, None)),
        check_vma=False,
    )
```

```python
from functools import partial

import jax
import jax.numpy as jnp
from jax import lax
from jax.sharding import PartitionSpec as P

H = 16
KEY_VALUE_HEADS = 4
DH = 128
BLK = 64


NEG_FILL = -1e30


def passed_along(array, axis, by):
    devices = lax.axis_size(axis)
    pairs = [(i, i + by) for i in range(devices) if 0 <= i + by < devices]
    return lax.ppermute(array, axis, pairs)


def head_scores(key_mask, queries, key_rows):
    raw = jnp.einsum(
        "bighd,gbnd->bighn", queries, key_rows, preferred_element_type=jnp.float32
    ) * DH ** (-0.5)
    return jnp.where(key_mask[:, :, None, None, :], raw, NEG_FILL)


def head_forward(key_mask, pieces):
    queries, key_rows, value_rows = pieces
    scores = head_scores(key_mask, queries, key_rows)
    row_max = jnp.max(scores, axis=-1, keepdims=True)
    log_total = row_max + jnp.log(jnp.sum(jnp.exp(scores - row_max), axis=-1, keepdims=True))
    prob_bf = jnp.exp(scores - log_total).astype(jnp.bfloat16)
    attended = jnp.einsum(
        "bighn,gbnd->bighd", prob_bf, value_rows, preferred_element_type=jnp.float32
    ).astype(jnp.bfloat16)
    return (log_total, attended)


def head_backward(key_mask, pieces):
    queries, key_rows, value_rows, grad_rows, log_total, attended = pieces
    scores = head_scores(key_mask, queries, key_rows)
    weights = jnp.exp(scores - log_total)
    prob_bf = weights.astype(jnp.bfloat16)
    dprobs = jnp.einsum("bighd,gbnd->bighn", grad_rows, value_rows, preferred_element_type=jnp.float32)
    row_delta = jnp.sum(
        grad_rows.astype(jnp.float32) * attended.astype(jnp.float32), axis=-1, keepdims=True
    )
    dscores = (weights * (dprobs - row_delta)).astype(jnp.bfloat16)
    inv_root = DH ** (-0.5)
    grad_query = (
        jnp.einsum("bighn,gbnd->bighd", dscores, key_rows, preferred_element_type=jnp.float32)
        * inv_root
    )
    grad_key = (
        jnp.einsum("bighn,bighd->bngd", dscores, queries, preferred_element_type=jnp.float32)
        * inv_root
    )
    grad_value = jnp.einsum(
        "bighn,bighd->bngd", prob_bf, grad_rows, preferred_element_type=jnp.float32
    )
    return (grad_query, grad_key, grad_value)


def masks(slot_live, owner_shard, tokens):
    qblocks, topk = owner_shard.shape
    memory_len = topk * BLK
    live_len = jnp.take(slot_live, owner_shard.reshape(-1))
    live_mask = (jnp.arange(BLK)[None, :] < live_len[:, None]).reshape(qblocks, memory_len)
    row_pos = jnp.arange(qblocks)[:, None] * BLK + jnp.arange(BLK)[None, :]
    causal = jnp.arange(tokens)[None, None, :] <= row_pos[:, :, None]
    return jnp.concatenate(
        [jnp.broadcast_to(live_mask[:, None, :], (qblocks, BLK, memory_len)), causal], axis=-1
    )


def per_device(qkv_rows, grad_output, memory_rows, shard_fill, block_ids):
    shards = lax.axis_size("mem")
    groups = H // KEY_VALUE_HEADS
    rows_here = qkv_rows[0, 0]
    tokens = rows_here.shape[0]
    ids_here = block_ids[0, 0]
    qblocks, topk = ids_here.shape
    memory_len = topk * BLK
    held_blocks = memory_rows.shape[1]
    queries = rows_here[:, : H * DH].reshape(qblocks, BLK, KEY_VALUE_HEADS, groups, DH)
    keys_local = rows_here[:, H * DH : (H + KEY_VALUE_HEADS) * DH].reshape(
        tokens, KEY_VALUE_HEADS, DH
    )
    values_local = rows_here[:, (H + KEY_VALUE_HEADS) * DH :].reshape(tokens, KEY_VALUE_HEADS, DH)
    grad_rows = grad_output[0, 0].reshape(qblocks, BLK, KEY_VALUE_HEADS, groups, DH)
    owner_shard = ids_here // held_blocks
    slot_index = ids_here % held_blocks
    shard_ids = jnp.arange(shards, dtype=jnp.int32)
    hits = owner_shard[:, :, None] == shard_ids[None, None, :]
    request = jnp.max(jnp.where(hits, slot_index[:, :, None], -1), axis=(0, 1))
    lanes = jnp.arange(128)[None, :]
    asks = jnp.where(lanes == 0, request[:, None], shard_fill[0, 0])
    answers = lax.all_to_all(asks, "mem", split_axis=0, concat_axis=0, tiled=True)
    wanted = answers[:, 0]
    fills = answers[:, 1]
    slot_live = jnp.where(request >= 0, jnp.clip(fills - request * BLK, 0, BLK), 0)
    key_mask = masks(slot_live, owner_shard, tokens)
    memory_here = memory_rows[0]
    width = KEY_VALUE_HEADS * DH
    wanted_hot = (wanted[:, None] == jnp.arange(held_blocks, dtype=jnp.int32)[None, :]).astype(
        jnp.bfloat16
    )
    owner_flat = owner_shard.reshape(-1)
    key_slot = jnp.sum(jnp.where(hits, jnp.arange(topk, dtype=jnp.int32)[None, :, None], 0), axis=1)
    present = jnp.any(hits, axis=1)
    per_chunk = 2
    chunks = KEY_VALUE_HEADS // per_chunk
    span = per_chunk * DH
    query_parts, key_parts, value_parts, owned_parts, sent_grads = [], [], [], [], []
    for chunk in range(chunks):
        first = chunk * per_chunk
        lo = first * DH
        memory_chunk = jnp.concatenate(
            [memory_here[:, :, lo : lo + span], memory_here[:, :, width + lo : width + lo + span]],
            axis=-1,
        )
        payload = memory_chunk.at[jnp.maximum(wanted, 0)].get(mode="promise_in_bounds")
        if chunk >= 2:
            payload, sent_grads[chunk - 2] = lax.optimization_barrier(
                (payload, sent_grads[chunk - 2])
            )
        slots = lax.all_to_all(payload, "mem", split_axis=0, concat_axis=0, tiled=True)
        if chunk >= 1:
            slots, sent_grads[chunk - 1] = lax.optimization_barrier(
                (slots, sent_grads[chunk - 1])
            )
        chosen = slots.at[owner_flat].get(mode="promise_in_bounds").reshape(
            qblocks, memory_len, 2, per_chunk, DH
        )
        mem_keys = jnp.transpose(chosen[:, :, 0], (2, 0, 1, 3))
        mem_values = jnp.transpose(chosen[:, :, 1], (2, 0, 1, 3))
        local_keys = jnp.transpose(keys_local[:, first : first + per_chunk], (1, 0, 2))
        local_values = jnp.transpose(values_local[:, first : first + per_chunk], (1, 0, 2))
        key_rows = jnp.concatenate(
            [mem_keys, jnp.broadcast_to(local_keys[:, None], (per_chunk, qblocks, tokens, DH))],
            axis=2,
        )
        value_rows = jnp.concatenate(
            [mem_values, jnp.broadcast_to(local_values[:, None], (per_chunk, qblocks, tokens, DH))],
            axis=2,
        )
        queries_chunk = queries[:, :, first : first + per_chunk]
        grads_chunk = grad_rows[:, :, first : first + per_chunk]
        log_total, attended = head_forward(key_mask, (queries_chunk, key_rows, value_rows))
        grad_query, grad_key, grad_value = head_backward(
            key_mask,
            (queries_chunk, key_rows, value_rows, grads_chunk, log_total, attended),
        )
        query_parts.append(grad_query.reshape(tokens, per_chunk * groups * DH))
        key_parts.append(jnp.sum(grad_key[:, memory_len:], axis=0).reshape(tokens, span))
        value_parts.append(jnp.sum(grad_value[:, memory_len:], axis=0).reshape(tokens, span))
        entry_grads = jnp.concatenate(
            [
                grad_key[:, :memory_len].reshape(qblocks * topk, BLK, span),
                grad_value[:, :memory_len].reshape(qblocks * topk, BLK, span),
            ],
            axis=-1,
        )
        by_block = entry_grads.reshape(qblocks, topk, BLK, 2 * span)
        slot_grads = sum(
            jnp.where(
                present[block][:, None, None],
                by_block[block].at[key_slot[block]].get(mode="promise_in_bounds"),
                jnp.float32(0.0),
            )
            for block in range(qblocks)
        ).astype(jnp.bfloat16)
        sent_grads.append(slot_grads)
    for chunk in range(chunks):
        received = lax.all_to_all(
            sent_grads[chunk], "mem", split_axis=0, concat_axis=0, tiled=True
        )
        owned = jnp.einsum(
            "rj,rtx->jtx", wanted_hot, received, preferred_element_type=jnp.float32
        )
        partner = lax.ppermute(owned, "dp", [(0, 1), (1, 0)])
        owned_parts.append(owned + partner)
    section_grads = jnp.concatenate(query_parts + key_parts + value_parts, axis=-1).astype(
        jnp.bfloat16
    )
    sections = lax.axis_size("section")
    cycled = lax.ppermute(
        section_grads, "section", [(i, (i - 1) % sections) for i in range(sections)]
    )
    last = lax.axis_index("section") == sections - 1
    upstream = jnp.where(last, jnp.zeros_like(cycled), cycled)[None, None]
    summed = jnp.concatenate(
        [part[:, :, :span] for part in owned_parts] + [part[:, :, span:] for part in owned_parts],
        axis=-1,
    )
    memory_grad = summed.astype(jnp.bfloat16)[None]
    return (upstream, memory_grad)


def solution(mesh):
    placed = (
        P("section", ("dp", "mem"), None, None),
        P("section", ("dp", "mem"), None, None),
        P("section", "mem", None, None),
        P("section", "mem"),
        P("section", ("dp", "mem"), None, None),
    )
    return jax.shard_map(
        per_device,
        mesh=mesh,
        in_specs=placed,
        out_specs=(P("section", ("dp", "mem"), None, None), P("section", "mem", None, None)),
        check_vma=False,
    )
```

```python
from functools import partial

import jax
import jax.numpy as jnp
from jax import lax
from jax.sharding import PartitionSpec as P

H = 16
KEY_VALUE_HEADS = 4
DH = 128
BLK = 64


NEG_FILL = -1e30


def passed_along(array, axis, by):
    devices = lax.axis_size(axis)
    pairs = [(i, i + by) for i in range(devices) if 0 <= i + by < devices]
    return lax.ppermute(array, axis, pairs)


def head_scores(key_mask, queries, key_rows):
    raw = jnp.einsum(
        "bighd,gbnd->bighn", queries, key_rows, preferred_element_type=jnp.float32
    ) * DH ** (-0.5)
    return jnp.where(key_mask[:, :, None, None, :], raw, NEG_FILL)


def head_forward(key_mask, pieces):
    queries, key_rows, value_rows = pieces
    scores = head_scores(key_mask, queries, key_rows)
    row_max = jnp.max(scores, axis=-1, keepdims=True)
    log_total = row_max + jnp.log(jnp.sum(jnp.exp(scores - row_max), axis=-1, keepdims=True))
    prob_bf = jnp.exp(scores - log_total).astype(jnp.bfloat16)
    attended = jnp.einsum(
        "bighn,gbnd->bighd", prob_bf, value_rows, preferred_element_type=jnp.float32
    ).astype(jnp.bfloat16)
    return (log_total, attended)


def head_backward(key_mask, pieces):
    queries, key_rows, value_rows, grad_rows, log_total, attended = pieces
    scores = head_scores(key_mask, queries, key_rows)
    weights = jnp.exp(scores - log_total)
    prob_bf = weights.astype(jnp.bfloat16)
    dprobs = jnp.einsum("bighd,gbnd->bighn", grad_rows, value_rows, preferred_element_type=jnp.float32)
    row_delta = jnp.sum(
        grad_rows.astype(jnp.float32) * attended.astype(jnp.float32), axis=-1, keepdims=True
    )
    dscores = (weights * (dprobs - row_delta)).astype(jnp.bfloat16)
    inv_root = DH ** (-0.5)
    grad_query = (
        jnp.einsum("bighn,gbnd->bighd", dscores, key_rows, preferred_element_type=jnp.float32)
        * inv_root
    )
    grad_key = (
        jnp.einsum("bighn,bighd->bngd", dscores, queries, preferred_element_type=jnp.float32)
        * inv_root
    )
    grad_value = jnp.einsum(
        "bighn,bighd->bngd", prob_bf, grad_rows, preferred_element_type=jnp.float32
    )
    return (grad_query, grad_key, grad_value)


def masks(slot_live, owner_shard, tokens):
    qblocks, topk = owner_shard.shape
    memory_len = topk * BLK
    live_len = jnp.take(slot_live, owner_shard.reshape(-1))
    live_mask = (jnp.arange(BLK)[None, :] < live_len[:, None]).reshape(qblocks, memory_len)
    row_pos = jnp.arange(qblocks)[:, None] * BLK + jnp.arange(BLK)[None, :]
    causal = jnp.arange(tokens)[None, None, :] <= row_pos[:, :, None]
    return jnp.concatenate(
        [jnp.broadcast_to(live_mask[:, None, :], (qblocks, BLK, memory_len)), causal], axis=-1
    )


def per_device(qkv_rows, grad_output, memory_rows, shard_fill, block_ids):
    shards = lax.axis_size("mem")
    groups = H // KEY_VALUE_HEADS
    rows_here = qkv_rows[0, 0]
    tokens = rows_here.shape[0]
    ids_here = block_ids[0, 0]
    qblocks, topk = ids_here.shape
    memory_len = topk * BLK
    held_blocks = memory_rows.shape[1]
    queries = rows_here[:, : H * DH].reshape(qblocks, BLK, KEY_VALUE_HEADS, groups, DH)
    keys_local = rows_here[:, H * DH : (H + KEY_VALUE_HEADS) * DH].reshape(
        tokens, KEY_VALUE_HEADS, DH
    )
    values_local = rows_here[:, (H + KEY_VALUE_HEADS) * DH :].reshape(tokens, KEY_VALUE_HEADS, DH)
    grad_rows = grad_output[0, 0].reshape(qblocks, BLK, KEY_VALUE_HEADS, groups, DH)
    owner_shard = ids_here // held_blocks
    slot_index = ids_here % held_blocks
    shard_ids = jnp.arange(shards, dtype=jnp.int32)
    hits = owner_shard[:, :, None] == shard_ids[None, None, :]
    request = jnp.max(jnp.where(hits, slot_index[:, :, None], -1), axis=(0, 1))
    asks = jnp.stack([request, jnp.broadcast_to(shard_fill[0, 0], (shards,))], axis=1)
    answers = lax.all_to_all(asks, "mem", split_axis=0, concat_axis=0, tiled=True)
    wanted = answers[:, 0]
    fills = answers[:, 1]
    slot_live = jnp.where(request >= 0, jnp.clip(fills - request * BLK, 0, BLK), 0)
    key_mask = masks(slot_live, owner_shard, tokens)
    memory_here = memory_rows[0]
    width = KEY_VALUE_HEADS * DH
    wanted_hot = (wanted[:, None] == jnp.arange(held_blocks, dtype=jnp.int32)[None, :]).astype(
        jnp.bfloat16
    )
    owner_flat = owner_shard.reshape(-1)
    key_slot = jnp.sum(jnp.where(hits, jnp.arange(topk, dtype=jnp.int32)[None, :, None], 0), axis=1)
    present = jnp.any(hits, axis=1)
    per_chunk = 2
    chunks = KEY_VALUE_HEADS // per_chunk
    span = per_chunk * DH
    query_parts, key_parts, value_parts, owned_parts, sent_grads = [], [], [], [], []
    for chunk in range(chunks):
        first = chunk * per_chunk
        lo = first * DH
        memory_chunk = jnp.concatenate(
            [memory_here[:, :, lo : lo + span], memory_here[:, :, width + lo : width + lo + span]],
            axis=-1,
        )
        payload = memory_chunk.at[jnp.maximum(wanted, 0)].get(mode="promise_in_bounds")
        if chunk >= 2:
            payload, sent_grads[chunk - 2] = lax.optimization_barrier(
                (payload, sent_grads[chunk - 2])
            )
        slots = lax.all_to_all(payload, "mem", split_axis=0, concat_axis=0, tiled=True)
        if chunk >= 1:
            slots, sent_grads[chunk - 1] = lax.optimization_barrier(
                (slots, sent_grads[chunk - 1])
            )
        chosen = slots.at[owner_flat].get(mode="promise_in_bounds").reshape(
            qblocks, memory_len, 2, per_chunk, DH
        )
        mem_keys = jnp.transpose(chosen[:, :, 0], (2, 0, 1, 3))
        mem_values = jnp.transpose(chosen[:, :, 1], (2, 0, 1, 3))
        local_keys = jnp.transpose(keys_local[:, first : first + per_chunk], (1, 0, 2))
        local_values = jnp.transpose(values_local[:, first : first + per_chunk], (1, 0, 2))
        key_rows = jnp.concatenate(
            [mem_keys, jnp.broadcast_to(local_keys[:, None], (per_chunk, qblocks, tokens, DH))],
            axis=2,
        )
        value_rows = jnp.concatenate(
            [mem_values, jnp.broadcast_to(local_values[:, None], (per_chunk, qblocks, tokens, DH))],
            axis=2,
        )
        queries_chunk = queries[:, :, first : first + per_chunk]
        grads_chunk = grad_rows[:, :, first : first + per_chunk]
        log_total, attended = head_forward(key_mask, (queries_chunk, key_rows, value_rows))
        grad_query, grad_key, grad_value = head_backward(
            key_mask,
            (queries_chunk, key_rows, value_rows, grads_chunk, log_total, attended),
        )
        query_parts.append(grad_query.reshape(tokens, per_chunk * groups * DH))
        key_parts.append(jnp.sum(grad_key[:, memory_len:], axis=0).reshape(tokens, span))
        value_parts.append(jnp.sum(grad_value[:, memory_len:], axis=0).reshape(tokens, span))
        entry_grads = jnp.concatenate(
            [
                grad_key[:, :memory_len].reshape(qblocks * topk, BLK, span),
                grad_value[:, :memory_len].reshape(qblocks * topk, BLK, span),
            ],
            axis=-1,
        )
        by_block = entry_grads.reshape(qblocks, topk, BLK, 2 * span)
        slot_grads = sum(
            jnp.where(
                present[block][:, None, None],
                by_block[block].at[key_slot[block]].get(mode="promise_in_bounds"),
                jnp.float32(0.0),
            )
            for block in range(qblocks)
        ).astype(jnp.bfloat16)
        sent_grads.append(slot_grads)
    for chunk in range(chunks):
        received = lax.all_to_all(
            sent_grads[chunk], "mem", split_axis=0, concat_axis=0, tiled=True
        )
        owned = jnp.einsum(
            "rj,rtx->jtx", wanted_hot, received, preferred_element_type=jnp.float32
        )
        if chunk + 1 == chunks:
            owned = owned.astype(jnp.bfloat16)
        partner = lax.ppermute(owned, "dp", [(0, 1), (1, 0)])
        owned_parts.append(owned.astype(jnp.float32) + partner.astype(jnp.float32))
    section_grads = jnp.concatenate(query_parts + key_parts + value_parts, axis=-1).astype(
        jnp.bfloat16
    )
    sections = lax.axis_size("section")
    cycled = lax.ppermute(
        section_grads, "section", [(i, (i - 1) % sections) for i in range(sections)]
    )
    last = lax.axis_index("section") == sections - 1
    upstream = jnp.where(last, jnp.zeros_like(cycled), cycled)[None, None]
    summed = jnp.concatenate(
        [part[:, :, :span] for part in owned_parts] + [part[:, :, span:] for part in owned_parts],
        axis=-1,
    )
    memory_grad = summed.astype(jnp.bfloat16)[None]
    return (upstream, memory_grad)


def solution(mesh):
    placed = (
        P("section", ("dp", "mem"), None, None),
        P("section", ("dp", "mem"), None, None),
        P("section", "mem", None, None),
        P("section", "mem"),
        P("section", ("dp", "mem"), None, None),
    )
    return jax.shard_map(
        per_device,
        mesh=mesh,
        in_specs=placed,
        out_specs=(P("section", ("dp", "mem"), None, None), P("section", "mem", None, None)),
        check_vma=False,
    )
```
